512 devices in a mesh: group: 8 (over x, core), dev: 64 (over y, z).
Axes of the slice: x: 4, y: 4, z: 16, core: 2. Of those that a mesh axis runs over, the one named last changes fastest.
Arguments:
- probes: bfloat16 [2048, 32, 1024], P(('group', 'dev')), may hold values from -6 to 6
- points: float32 [2048, 3, 1024], P(('group', 'dev')), may hold values from -2.5 to 5.5
- leaf_order: int32 [2048, 1024], P(('group', 'dev')), may hold values from 0 to 1023, each once within a row
- leaf_basis: bfloat16 [2048, 1024, 256], P(('group', 'dev')), may hold values from -0.1875 to 0.1875
- node_transfer: bfloat16 [512, 4, 256, 256], P(('group', 'dev')), may hold values from -0.375 to 0.375
- group_transfer: bfloat16 [512, 256, 256], P(('group', 'dev')), may hold values from -0.375 to 0.375
- node_skeleton: float32 [512, 3, 256], P('group'), may hold values from 0 to 2
- group_skeleton: float32 [8, 3, 256], replicated, may hold values from 0 to 8
- near_pattern: int32 [2048, 5], P(('group', 'dev')), may hold values from 0 to 1, as said below
- node_coupling: int32 [512, 9], P(('group', 'dev')), may hold values 0 or 1
- signal_variance: float32 [], replicated, may hold values from 0.1 to 0.25
- noise_variance: float32 [], replicated, may hold values from 0.5 to 1.5
Outputs:
- applied: bfloat16 [2048, 32, 1024], P(('group', 'dev'))
The draws below stay inside these ranges and needn't reach their ends.
Inputs may be any that keep to these rules, and one draw needn't show every extreme that they name: `leaf_order`: each row is a permutation. `near_pattern`: 1 marks a near-field block with the leaf at that offset; entries for leaves outside the set are not used. `node_coupling`: 1 marks a coupling with the node at that offset; entries with offsets under 2 or nodes outside the subtree are not used.
All inputs are finite; a program needn't handle non-finite values. No bound on the sum of `node_coupling` on one device may be relied on, other than what follows from the above.
Results may differ from the reference program's by a relative error of at most 0.012.
Values may be sent and summed in bfloat16 or wider, within the bound.
No kernel may reach another device: no remote copies, remote signals or barrier semaphores. Data moves between devices by JAX's collectives and lax.ppermute only.
A program may use at most 64 MiB of HBM per device.

```python
import math
import jax
import jax.numpy as jnp
from jax import lax

LEAF_SIZE = 1024
SKELETON = 256
PROBES = 32
NEAR_REACH = 2
COUPLE_REACH = 4
LEAVES_DEV = 4
LEAVES = 2048
TREE_NODES = 512
GROUPS = 8
N_DEV = 64


def draw_points(key, part):
    first = jax.random.fold_in(key, 11)
    second = jax.random.fold_in(key, 12)
    third = jax.random.fold_in(key, 13)
    radius = 2.0
    band = 0.3
    along = (jnp.arange(LEAVES, dtype=jnp.float32) + 0.5) * (3.0 / LEAVES)
    jitter = jax.random.uniform(third, (LEAVES,), jnp.float32, -0.05, 0.05)
    sideways = jax.random.uniform(first, (LEAVES, 2), jnp.float32, 1.5 - band, 1.5 + band)
    centres = jnp.concatenate([(along + jitter)[:, None], sideways], axis=1)[:, :, None]
    spread = jax.random.uniform(second, (LEAVES, 3, LEAF_SIZE), jnp.float32, -radius, radius)
    return jnp.clip(centres + spread, -2.5, 5.5)


def draw_near_pattern(key, part):
    first = jax.random.fold_in(key, 21)
    second = jax.random.fold_in(key, 22)
    levels = jax.random.randint(first, (TREE_NODES, 1, 1), 1, 5)
    rolls = jax.random.randint(second, (TREE_NODES, LEAVES_DEV, 2 * NEAR_REACH + 1), 0, 4)
    marks = jnp.where(rolls < levels, 1, 0).astype(jnp.int32)
    return marks.reshape(LEAVES, 2 * NEAR_REACH + 1)


def set_ends(values, own_key, least, largest):
    longest = values.shape.index(max(values.shape))
    spots = []
    for shift in (0, 1):
        where = [jax.random.randint(jax.random.fold_in(own_key, axis), (), 0, length) for axis, length in enumerate(values.shape)]
        where[longest] = (where[longest] + shift) % values.shape[longest]
        spots.append(tuple(where))
    return values.at[spots[0]].set(least).at[spots[1]].set(largest)


def block_levels(own_key, extent, shards, least, largest):
    factor_of, own = 1.0, jax.random.fold_in(own_key, 6)
    for dim, shards_of in shards:
        steps = jnp.exp(jax.random.uniform(jax.random.fold_in(own, dim), (shards_of,), jnp.float32, least / len(shards), largest / len(shards)))
        factor_of = factor_of * jnp.repeat(steps, extent[dim] // shards_of).reshape([-1 if axis == dim else 1 for axis in range(len(extent))])
    return factor_of


def gaussian(own_key, dims, deviation, most, pieces=(), held_as=jnp.bfloat16):
    values = jax.random.normal(own_key, dims, jnp.float32) * deviation
    if len(pieces) > 0:
        values = block_levels(own_key, dims, pieces, -0.22, 0.18) * values
    return jnp.clip(values, min=-most, max=most).astype(held_as)


def setup_inputs(seed: int = 0) -> dict:
    key_of = jax.random.split(jax.random.key(seed), 13)
    return {
        "probes": gaussian(key_of[0], (LEAVES, PROBES, LEAF_SIZE), 1.0, 6.0, ((0, 512),)),
        "points": draw_points(jax.random.fold_in(key_of[12], 71), 0),
        "leaf_order": jax.vmap(lambda own: jax.random.permutation(own, LEAF_SIZE))(jax.random.split(key_of[2], LEAVES)).reshape((LEAVES, LEAF_SIZE)).astype(jnp.int32),
        "leaf_basis": gaussian(key_of[3], (LEAVES, LEAF_SIZE, SKELETON), LEAF_SIZE ** -0.5, 0.1875, ((0, 512),)),
        "node_transfer": gaussian(key_of[4], (TREE_NODES, LEAVES_DEV, SKELETON, SKELETON), SKELETON ** -0.5, 0.375, ((0, 512),)),
        "group_transfer": gaussian(key_of[5], (TREE_NODES, SKELETON, SKELETON), SKELETON ** -0.5, 0.375, ((0, 512),)),
        "node_skeleton": jnp.clip(2.0 * jax.random.uniform(key_of[6], (TREE_NODES, 3, SKELETON), jnp.float32) ** block_levels(key_of[6], (TREE_NODES, 3, SKELETON), ((0, 8),), -0.2, 0.2), 0.0, 2.0),
        "group_skeleton": jnp.clip(jax.random.uniform(key_of[7], (GROUPS, 3, SKELETON), jnp.float32, 0.0, 8.0), 0.0, 8.0),
        "near_pattern": draw_near_pattern(jax.random.fold_in(key_of[12], 71), 0),
        "node_coupling": set_ends((jax.random.randint(key_of[9], (TREE_NODES, 2 * COUPLE_REACH + 1), 0, 2) < 1).astype(jnp.int32), jax.random.fold_in(key_of[9], 1), 0, 1),
        "signal_variance": jnp.clip(jnp.exp(jax.random.uniform(key_of[10], (), jnp.float32, math.log(0.1), math.log(0.25))), 0.1, 0.25),
        "noise_variance": jnp.clip(jax.random.uniform(key_of[11], (), jnp.float32, 0.5, 1.5), 0.5, 1.5),
    }


ROOT_THREE = 1.7320508075688772
LENGTH_SCALE = 0.5

def matern(source, target, amplitude):
    square = (source[0][:, None] - target[0][None, :]) ** 2
    square = square + (source[1][:, None] - target[1][None, :]) ** 2
    square = square + (source[2][:, None] - target[2][None, :]) ** 2
    scaled = jnp.sqrt(square) * (ROOT_THREE / LENGTH_SCALE)
    return (amplitude * (1.0 + scaled) * jnp.exp(-scaled)).astype(jnp.bfloat16)

def reference(probes, points, leaf_order, leaf_basis, node_transfer, group_transfer, node_skeleton, group_skeleton, near_pattern, node_coupling, signal_variance, noise_variance):
    ordered = jnp.take_along_axis(probes, leaf_order[:, None, :], axis=2)
    window = 2 * NEAR_REACH + 1

    def near_leaf(position):
        target = points[position]
        summed = jnp.zeros((PROBES, LEAF_SIZE), jnp.float32)
        for offset in range(window):
            source = position + offset - NEAR_REACH
            usable = (source >= 0) & (source < LEAVES) & (near_pattern[position, offset] > 0)
            clamped = jnp.clip(source, 0, LEAVES - 1).astype(jnp.int32)
            kernel_tile = matern(points[clamped], target, signal_variance)
            contribution = jnp.dot(ordered[clamped], kernel_tile, preferred_element_type=jnp.float32)
            summed = summed + jnp.where(usable, contribution, jnp.float32(0.0))
        return summed
    near = lax.map(near_leaf, jnp.arange(LEAVES, dtype=jnp.int32))

    def lift_leaf(item):
        values, basis = item
        return jnp.dot(values, basis, preferred_element_type=jnp.float32).astype(jnp.bfloat16)
    leaf_coef = lax.map(lift_leaf, (ordered, leaf_basis))
    leaf_nodes = leaf_coef.reshape(TREE_NODES, LEAVES_DEV, PROBES, SKELETON)

    def lift_node(item):
        coefs, transfer = item
        stacked = coefs.transpose(1, 0, 2).reshape(PROBES, LEAVES_DEV * SKELETON)
        return jnp.dot(stacked, transfer.reshape(LEAVES_DEV * SKELETON, SKELETON), preferred_element_type=jnp.float32).astype(jnp.bfloat16)
    node_coef = lax.map(lift_node, (leaf_nodes, node_transfer))

    def root_term(item):
        coefs, transfer = item
        return jnp.dot(coefs, transfer, preferred_element_type=jnp.float32)
    group_terms = lax.map(root_term, (node_coef, group_transfer))
    group_coef = group_terms.reshape(GROUPS, N_DEV, PROBES, SKELETON).sum(axis=1).astype(jnp.bfloat16)
    group_rows = []
    for target_group in range(GROUPS):
        summed = jnp.zeros((PROBES, SKELETON), jnp.float32)
        for other in range(GROUPS):
            if other != target_group:
                kernel_tile = matern(group_skeleton[other], group_skeleton[target_group], signal_variance)
                summed = summed + jnp.dot(group_coef[other], kernel_tile, preferred_element_type=jnp.float32)
        group_rows.append(summed.astype(jnp.bfloat16))
    group_local = jnp.stack(group_rows)

    def down_node(node):
        local = node % N_DEV
        own_node = node_skeleton[node]
        far_node = jnp.zeros((PROBES, SKELETON), jnp.float32)
        for offset in range(-COUPLE_REACH, COUPLE_REACH + 1):
            if abs(offset) < 2:
                continue
            partner = local + offset
            usable = (partner >= 0) & (partner < N_DEV) & (node_coupling[node, offset + COUPLE_REACH] > 0)
            clamped = jnp.clip(node + offset, 0, TREE_NODES - 1).astype(jnp.int32)
            kernel_tile = matern(node_skeleton[clamped], own_node, signal_variance)
            contribution = jnp.dot(node_coef[clamped], kernel_tile, preferred_element_type=jnp.float32)
            far_node = far_node + jnp.where(usable, contribution, jnp.float32(0.0))
        pushed = lax.dot_general(group_local[node // N_DEV], group_transfer[node], (((1,), (1,)), ((), ())), preferred_element_type=jnp.float32)
        node_local = (pushed + far_node).astype(jnp.bfloat16)
        spread = lax.dot_general(node_local, node_transfer[node].reshape(LEAVES_DEV * SKELETON, SKELETON), (((1,), (1,)), ((), ())), preferred_element_type=jnp.float32)
        return spread.reshape(PROBES, LEAVES_DEV, SKELETON).transpose(1, 0, 2).astype(jnp.bfloat16)
    leaf_local = lax.map(down_node, jnp.arange(TREE_NODES, dtype=jnp.int32)).reshape(LEAVES, PROBES, SKELETON)

    def finish_leaf(item):
        local_coef, basis, near_term, values, ordering = item
        far_term = lax.dot_general(local_coef, basis, (((1,), (1,)), ((), ())), preferred_element_type=jnp.float32)
        result = far_term + near_term + noise_variance * values.astype(jnp.float32)
        restored = jnp.zeros_like(result).at[:, ordering].set(result)
        return restored.astype(jnp.bfloat16)
    return lax.map(finish_leaf, (leaf_local, leaf_basis, near, ordered, leaf_order))
```

```python
import jax
import jax.numpy as jnp
from jax import lax
from jax.sharding import Mesh
from jax.sharding import PartitionSpec as P

NEAR_REACH = 2
COUPLE_REACH = 4
GROUP_DEV = ("group", "dev_0", "dev_1")
DEV = ("dev_0", "dev_1")


ROOT_THREE = 1.7320508075688772
LENGTH_SCALE = 0.5


def with_halo(value, axis, width):
    peers, length = (lax.axis_size(axis), value.shape[0])
    up = [(i, i + 1) for i in range(peers - 1)]
    last = value[length - width :]
    leading = value[:width]
    low = lax.ppermute(last, axis, up)
    high = lax.ppermute(leading, axis, [(b, a) for a, b in up])
    return jnp.concatenate([low, value, high], axis=0)


def from_behind(block, axis, distance):
    devices = range(lax.axis_size(axis))
    route = [(i - distance, i) for i in devices if i - distance in devices]
    return lax.ppermute(block, axis, route)


def matern(source, target, amplitude):
    square = (source[0][:, None] - target[0][None, :]) ** 2
    square = square + (source[1][:, None] - target[1][None, :]) ** 2
    square = square + (source[2][:, None] - target[2][None, :]) ** 2
    scaled = jnp.sqrt(square) * (ROOT_THREE / LENGTH_SCALE)
    return (amplitude * (1.0 + scaled) * jnp.exp(-scaled)).astype(jnp.bfloat16)


def one_hot(ordering, size):
    rows = lax.broadcasted_iota(jnp.int32, (size, size), 0)
    return (rows == ordering[None, :]).astype(jnp.bfloat16)


def on_device(
    probes,
    points,
    leaf_order,
    leaf_basis,
    node_transfer,
    group_transfer,
    node_skeleton,
    group_skeleton,
    near_pattern,
    node_coupling,
    signal_variance,
    noise_variance,
):
    leaf_count, probe_count, leaf_size = probes.shape
    skeleton = leaf_basis.shape[2]
    f32 = jnp.float32

    hots = [one_hot(leaf_order[i], leaf_size) for i in range(leaf_count)]
    ordered = jnp.stack(
        [
            jnp.dot(probes[i], hots[i], preferred_element_type=f32).astype(jnp.bfloat16)
            for i in range(leaf_count)
        ]
    )

    leaf_coef = lax.dot_general(
        ordered, leaf_basis, (((2,), (1,)), ((0,), (0,))), preferred_element_type=f32
    ).astype(jnp.bfloat16)
    stacked = leaf_coef.transpose(1, 0, 2).reshape(probe_count, leaf_count * skeleton)
    transfer_flat = node_transfer[0].reshape(leaf_count * skeleton, skeleton)
    node_coef = jnp.dot(stacked, transfer_flat, preferred_element_type=f32).astype(jnp.bfloat16)
    group_term = jnp.dot(node_coef, group_transfer[0], preferred_element_type=f32)
    own_coef = lax.psum(group_term, DEV).astype(jnp.bfloat16)
    group_coef = lax.all_gather(own_coef, "group", axis=0, tiled=False)

    node_index = lax.axis_index(DEV)
    node_total = lax.axis_size(DEV)
    relayed = {}
    for offset in range(-COUPLE_REACH, COUPLE_REACH + 1):
        if abs(offset) < 2:
            continue
        relayed[offset] = from_behind(node_coef, DEV, -offset)

    wide_probes = with_halo(ordered, GROUP_DEV, NEAR_REACH)
    wide_points = with_halo(points, GROUP_DEV, NEAR_REACH)
    wide = leaf_count + 2 * NEAR_REACH
    own = range(NEAR_REACH, NEAR_REACH + leaf_count)
    pattern = near_pattern.astype(f32)
    near = [jnp.zeros((probe_count, leaf_size), f32) for _ in range(leaf_count)]
    for b in own:
        tile = matern(wide_points[b], wide_points[b], signal_variance)
        t = b - NEAR_REACH
        near[t] = near[t] + jnp.dot(
            wide_probes[b], tile, preferred_element_type=f32
        ) * pattern[t, NEAR_REACH]
    for gap in range(1, NEAR_REACH + 1):
        for a in range(wide - gap):
            b = a + gap
            if a not in own and b not in own:
                continue
            tile = matern(wide_points[a], wide_points[b], signal_variance)
            if b in own:
                t = b - NEAR_REACH
                near[t] = near[t] + jnp.dot(
                    wide_probes[a], tile, preferred_element_type=f32
                ) * pattern[t, NEAR_REACH - gap]
            if a in own:
                t = a - NEAR_REACH
                near[t] = near[t] + lax.dot_general(
                    wide_probes[b], tile, (((1,), (1,)), ((), ())), preferred_element_type=f32
                ) * pattern[t, NEAR_REACH + gap]
    near = jnp.stack(near)

    group_index = lax.axis_index("group")
    group_total = lax.axis_size("group")
    own_skeleton = lax.dynamic_index_in_dim(group_skeleton, group_index, 0, keepdims=False)
    far_group = jnp.zeros((probe_count, skeleton), f32)
    for other in range(group_total):
        kernel_tile = matern(group_skeleton[other], own_skeleton, signal_variance)
        contribution = jnp.dot(group_coef[other], kernel_tile, preferred_element_type=f32)
        far_group = far_group + jnp.where(other != group_index, contribution, f32(0.0))
    group_local = far_group.astype(jnp.bfloat16)

    own_node = lax.dynamic_index_in_dim(node_skeleton, node_index, 0, keepdims=False)
    far_node = jnp.zeros((probe_count, skeleton), f32)
    for offset in range(-COUPLE_REACH, COUPLE_REACH + 1):
        if abs(offset) < 2:
            continue
        partner = node_index + offset
        usable = (
            (partner >= 0) & (partner < node_total) & (node_coupling[0, offset + COUPLE_REACH] > 0)
        )
        clamped = jnp.clip(partner, 0, node_total - 1)
        partner_points = lax.dynamic_index_in_dim(node_skeleton, clamped, 0, keepdims=False)
        kernel_tile = matern(partner_points, own_node, signal_variance)
        contribution = jnp.dot(relayed[offset], kernel_tile, preferred_element_type=f32)
        far_node = far_node + jnp.where(usable, contribution, f32(0.0))

    pushed = lax.dot_general(
        group_local, group_transfer[0], (((1,), (1,)), ((), ())), preferred_element_type=f32
    )
    node_local = (pushed + far_node).astype(jnp.bfloat16)
    spread = lax.dot_general(
        node_local, transfer_flat, (((1,), (1,)), ((), ())), preferred_element_type=f32
    )
    leaf_local = (
        spread.reshape(probe_count, leaf_count, skeleton).transpose(1, 0, 2).astype(jnp.bfloat16)
    )
    far_leaf = lax.dot_general(
        leaf_local, leaf_basis, (((2,), (2,)), ((0,), (0,))), preferred_element_type=f32
    )
    result = (far_leaf + near + noise_variance * ordered.astype(f32)).astype(jnp.bfloat16)
    restored = [
        lax.dot_general(
            result[i], hots[i], (((1,), (1,)), ((), ())), preferred_element_type=f32
        ).astype(jnp.bfloat16)
        for i in range(leaf_count)
    ]
    return jnp.stack(restored)


def solution(mesh):
    finer = Mesh(mesh.devices.reshape(mesh.shape["group"], 4, 16), ("group", "dev_0", "dev_1"))
    return jax.shard_map(
        on_device,
        mesh=finer,
        in_specs=(
            P(GROUP_DEV, None, None),
            P(GROUP_DEV, None, None),
            P(GROUP_DEV, None),
            P(GROUP_DEV, None, None),
            P(GROUP_DEV, None, None, None),
            P(GROUP_DEV, None, None),
            P("group", None, None),
            P(),
            P(GROUP_DEV, None),
            P(GROUP_DEV, None),
            P(),
            P(),
        ),
        out_specs=P(GROUP_DEV, None, None),
        check_vma=False,
    )
```

```python
import jax
import jax.numpy as jnp
from jax import lax
from jax.sharding import Mesh
from jax.sharding import PartitionSpec as P

NEAR_REACH = 2
COUPLE_REACH = 4
GROUP_DEV = ("group", "dev_0", "dev_1")
DEV = ("dev_0", "dev_1")


ROOT_THREE = 1.7320508075688772
LENGTH_SCALE = 0.5


def with_halo(value, axis, width):
    peers, length = (lax.axis_size(axis), value.shape[0])
    up = [(i, i + 1) for i in range(peers - 1)]
    last = value[length - width :]
    leading = value[:width]
    low = lax.ppermute(last, axis, up)
    high = lax.ppermute(leading, axis, [(b, a) for a, b in up])
    return jnp.concatenate([low, value, high], axis=0)


def from_behind(block, axis, distance):
    devices = range(lax.axis_size(axis))
    route = [(i - distance, i) for i in devices if i - distance in devices]
    return lax.ppermute(block, axis, route)


def tree_sum(value, axis):
    peers = lax.axis_size(axis)
    step = 1
    while step < peers:
        value = value + lax.ppermute(value, axis, [(i, i ^ step) for i in range(peers)])
        step *= 2
    return value


def cyclic_from_behind(block, axis, distance):
    peers = lax.axis_size(axis)
    return lax.ppermute(block, axis, [(i, (i + distance) % peers) for i in range(peers)])


def matern(source, target, amplitude):
    square = (source[0][:, None] - target[0][None, :]) ** 2
    square = square + (source[1][:, None] - target[1][None, :]) ** 2
    square = square + (source[2][:, None] - target[2][None, :]) ** 2
    scaled = jnp.sqrt(square) * (ROOT_THREE / LENGTH_SCALE)
    return (amplitude * (1.0 + scaled) * jnp.exp(-scaled)).astype(jnp.bfloat16)


def one_hot(ordering, size):
    rows = lax.broadcasted_iota(jnp.int32, (size, size), 0)
    return (rows == ordering[None, :]).astype(jnp.bfloat16)


def on_device(
    probes,
    points,
    leaf_order,
    leaf_basis,
    node_transfer,
    group_transfer,
    node_skeleton,
    group_skeleton,
    near_pattern,
    node_coupling,
    signal_variance,
    noise_variance,
):
    leaf_count, probe_count, leaf_size = probes.shape
    skeleton = leaf_basis.shape[2]
    f32 = jnp.float32

    hots = [one_hot(leaf_order[i], leaf_size) for i in range(leaf_count)]
    ordered = jnp.stack(
        [
            jnp.dot(probes[i], hots[i], preferred_element_type=f32).astype(jnp.bfloat16)
            for i in range(leaf_count)
        ]
    )

    leaf_coef = lax.dot_general(
        ordered, leaf_basis, (((2,), (1,)), ((0,), (0,))), preferred_element_type=f32
    ).astype(jnp.bfloat16)
    stacked = leaf_coef.transpose(1, 0, 2).reshape(probe_count, leaf_count * skeleton)
    transfer_flat = node_transfer[0].reshape(leaf_count * skeleton, skeleton)
    node_coef = jnp.dot(stacked, transfer_flat, preferred_element_type=f32).astype(jnp.bfloat16)
    group_term = jnp.dot(node_coef, group_transfer[0], preferred_element_type=f32)
    node_index = lax.axis_index(DEV)
    node_total = lax.axis_size(DEV)
    relayed = {}
    for offset in range(-COUPLE_REACH, COUPLE_REACH + 1):
        if abs(offset) < 2:
            continue
        relayed[offset] = from_behind(node_coef, DEV, -offset)

    wide_probes = with_halo(ordered, GROUP_DEV, NEAR_REACH)
    wide_points = with_halo(points, GROUP_DEV, NEAR_REACH)
    wide = leaf_count + 2 * NEAR_REACH
    own = range(NEAR_REACH, NEAR_REACH + leaf_count)
    pattern = near_pattern.astype(f32)
    jobs = [(b, b) for b in own]
    cross = []
    for gap in range(1, NEAR_REACH + 1):
        for a in range(wide - gap):
            b = a + gap
            if a in own and b in own:
                jobs.append((a, b))
            elif a in own or b in own:
                cross.append((a, b))
    jobs += cross
    near = [jnp.zeros((probe_count, leaf_size), f32) for _ in range(leaf_count)]

    def run_job(job, at, values):
        a, b = job
        tile = matern(at[a], at[b], signal_variance)
        if a == b:
            t = b - NEAR_REACH
            near[t] = near[t] + jnp.dot(values[b], tile, preferred_element_type=f32) * pattern[
                t, NEAR_REACH
            ]
            return
        gap = b - a
        if a in own and b in own:
            tile = lax.optimization_barrier(tile)
        if b in own:
            t = b - NEAR_REACH
            near[t] = near[t] + jnp.dot(
                values[a], tile, preferred_element_type=f32
            ) * pattern[t, NEAR_REACH - gap]
        if a in own:
            t = a - NEAR_REACH
            near[t] = near[t] + lax.dot_general(
                values[b], tile, (((1,), (1,)), ((), ())), preferred_element_type=f32
            ) * pattern[t, NEAR_REACH + gap]

    rounds = [("dev_1", 1), ("dev_1", 2), ("dev_1", 4), ("dev_1", 8), ("dev_0", 1), ("dev_0", 2)]
    steps = len(rounds) + 1
    running = group_term
    group_index = lax.axis_index("group")
    group_total = lax.axis_size("group")
    for step in range(steps):
        chunk = jobs[step * len(jobs) // steps : (step + 1) * len(jobs) // steps]
        if any(job in cross for job in chunk):
            running, at, values = lax.optimization_barrier((running, wide_points, wide_probes))
        else:
            running, at, values = lax.optimization_barrier((running, points, ordered))
            at = {b: at[b - NEAR_REACH] for b in own}
            values = {b: values[b - NEAR_REACH] for b in own}
        if step < len(rounds):
            axis, bit = rounds[step]
            peers = lax.axis_size(axis)
            received = lax.ppermute(running, axis, [(i, i ^ bit) for i in range(peers)])
        else:
            own_coef = running.astype(jnp.bfloat16)
            group_coef = {
                shift: cyclic_from_behind(own_coef, "group", shift)
                for shift in range(1, group_total)
            }
        for job in chunk:
            run_job(job, at, values)
        if step < len(rounds):
            running = running + received
    near = jnp.stack(near)

    own_skeleton = lax.dynamic_index_in_dim(group_skeleton, group_index, 0, keepdims=False)
    far_group = jnp.zeros((probe_count, skeleton), f32)
    for shift in range(1, group_total):
        other = (group_index - shift) % group_total
        other_skeleton = lax.dynamic_index_in_dim(group_skeleton, other, 0, keepdims=False)
        kernel_tile = matern(other_skeleton, own_skeleton, signal_variance)
        far_group = far_group + jnp.dot(group_coef[shift], kernel_tile, preferred_element_type=f32)
    group_local = far_group.astype(jnp.bfloat16)

    own_node = lax.dynamic_index_in_dim(node_skeleton, node_index, 0, keepdims=False)
    far_node = jnp.zeros((probe_count, skeleton), f32)
    for offset in range(-COUPLE_REACH, COUPLE_REACH + 1):
        if abs(offset) < 2:
            continue
        partner = node_index + offset
        usable = (
            (partner >= 0) & (partner < node_total) & (node_coupling[0, offset + COUPLE_REACH] > 0)
        )
        clamped = jnp.clip(partner, 0, node_total - 1)
        partner_points = lax.dynamic_index_in_dim(node_skeleton, clamped, 0, keepdims=False)
        kernel_tile = matern(partner_points, own_node, signal_variance)
        contribution = jnp.dot(relayed[offset], kernel_tile, preferred_element_type=f32)
        far_node = far_node + jnp.where(usable, contribution, f32(0.0))

    pushed = lax.dot_general(
        group_local, group_transfer[0], (((1,), (1,)), ((), ())), preferred_element_type=f32
    )
    node_local = (pushed + far_node).astype(jnp.bfloat16)
    spread = lax.dot_general(
        node_local, transfer_flat, (((1,), (1,)), ((), ())), preferred_element_type=f32
    )
    leaf_local = (
        spread.reshape(probe_count, leaf_count, skeleton).transpose(1, 0, 2).astype(jnp.bfloat16)
    )
    far_leaf = lax.dot_general(
        leaf_local, leaf_basis, (((2,), (2,)), ((0,), (0,))), preferred_element_type=f32
    )
    result = (far_leaf + near + noise_variance * ordered.astype(f32)).astype(jnp.bfloat16)
    restored = [
        lax.dot_general(
            result[i], hots[i], (((1,), (1,)), ((), ())), preferred_element_type=f32
        ).astype(jnp.bfloat16)
        for i in range(leaf_count)
    ]
    return jnp.stack(restored)


def solution(mesh):
    finer = Mesh(mesh.devices.reshape(mesh.shape["group"], 4, 16), ("group", "dev_0", "dev_1"))
    return jax.shard_map(
        on_device,
        mesh=finer,
        in_specs=(
            P(GROUP_DEV, None, None),
            P(GROUP_DEV, None, None),
            P(GROUP_DEV, None),
            P(GROUP_DEV, None, None),
            P(GROUP_DEV, None, None, None),
            P(GROUP_DEV, None, None),
            P("group", None, None),
            P(),
            P(GROUP_DEV, None),
            P(GROUP_DEV, None),
            P(),
            P(),
        ),
        out_specs=P(GROUP_DEV, None, None),
        check_vma=False,
    )
```

```python
import jax
import jax.numpy as jnp
from jax import lax
from jax.sharding import Mesh
from jax.sharding import PartitionSpec as P

NEAR_REACH = 2
COUPLE_REACH = 4
GROUP_DEV = ("group", "dev_0", "dev_1")
DEV = ("dev_0", "dev_1")


ROOT_THREE = 1.7320508075688772
LENGTH_SCALE = 0.5


def with_halo(value, axis, width):
    peers, length = (lax.axis_size(axis), value.shape[0])
    up = [(i, i + 1) for i in range(peers - 1)]
    last = value[length - width :]
    leading = value[:width]
    low = lax.ppermute(last, axis, up)
    high = lax.ppermute(leading, axis, [(b, a) for a, b in up])
    return jnp.concatenate([low, value, high], axis=0)


def from_behind(block, axis, distance):
    devices = range(lax.axis_size(axis))
    route = [(i - distance, i) for i in devices if i - distance in devices]
    return lax.ppermute(block, axis, route)


def tree_sum(value, axis):
    peers = lax.axis_size(axis)
    step = 1
    while step < peers:
        value = value + lax.ppermute(value, axis, [(i, i ^ step) for i in range(peers)])
        step *= 2
    return value


def cyclic_from_behind(block, axis, distance):
    peers = lax.axis_size(axis)
    return lax.ppermute(block, axis, [(i, (i + distance) % peers) for i in range(peers)])


def matern(source, target, amplitude):
    square = (source[0][:, None] - target[0][None, :]) ** 2
    square = square + (source[1][:, None] - target[1][None, :]) ** 2
    square = square + (source[2][:, None] - target[2][None, :]) ** 2
    scaled = jnp.sqrt(square) * (ROOT_THREE / LENGTH_SCALE)
    return (amplitude * (1.0 + scaled) * jnp.exp(-scaled)).astype(jnp.bfloat16)


def one_hot(ordering, size):
    rows = lax.broadcasted_iota(jnp.int32, (size, size), 0)
    return (rows == ordering[None, :]).astype(jnp.bfloat16)


def on_device(
    probes,
    points,
    leaf_order,
    leaf_basis,
    node_transfer,
    group_transfer,
    node_skeleton,
    group_skeleton,
    near_pattern,
    node_coupling,
    signal_variance,
    noise_variance,
):
    leaf_count, probe_count, leaf_size = probes.shape
    skeleton = leaf_basis.shape[2]
    f32 = jnp.float32

    hots = [one_hot(leaf_order[i], leaf_size) for i in range(leaf_count)]
    ordered = jnp.stack(
        [
            jnp.dot(probes[i], hots[i], preferred_element_type=f32).astype(jnp.bfloat16)
            for i in range(leaf_count)
        ]
    )

    leaf_coef = lax.dot_general(
        ordered, leaf_basis, (((2,), (1,)), ((0,), (0,))), preferred_element_type=f32
    ).astype(jnp.bfloat16)
    stacked = leaf_coef.transpose(1, 0, 2).reshape(probe_count, leaf_count * skeleton)
    transfer_flat = node_transfer[0].reshape(leaf_count * skeleton, skeleton)
    node_coef = jnp.dot(stacked, transfer_flat, preferred_element_type=f32).astype(jnp.bfloat16)
    group_term = jnp.dot(node_coef, group_transfer[0], preferred_element_type=f32)
    node_index = lax.axis_index(DEV)
    node_total = lax.axis_size(DEV)
    relayed = {}
    for offset in range(-COUPLE_REACH, COUPLE_REACH + 1):
        if abs(offset) < 2:
            continue
        relayed[offset] = from_behind(node_coef, DEV, -offset)

    wide_probes = with_halo(ordered, GROUP_DEV, NEAR_REACH)
    wide_points = with_halo(points, GROUP_DEV, NEAR_REACH)
    wide = leaf_count + 2 * NEAR_REACH
    own = range(NEAR_REACH, NEAR_REACH + leaf_count)
    pattern = near_pattern.astype(f32)
    jobs = [(b, b) for b in own]
    cross = []
    for gap in range(1, NEAR_REACH + 1):
        for a in range(wide - gap):
            b = a + gap
            if a in own and b in own:
                jobs.append((a, b))
            elif a in own or b in own:
                cross.append((a, b))
    jobs += cross
    near = [jnp.zeros((probe_count, leaf_size), f32) for _ in range(leaf_count)]

    def run_job(job, at, values):
        a, b = job
        tile = matern(at[a], at[b], signal_variance)
        if a == b:
            t = b - NEAR_REACH
            near[t] = near[t] + jnp.dot(values[b], tile, preferred_element_type=f32) * pattern[
                t, NEAR_REACH
            ]
            return
        gap = b - a
        if a in own and b in own:
            tile = lax.optimization_barrier(tile)
        if b in own:
            t = b - NEAR_REACH
            near[t] = near[t] + jnp.dot(
                values[a], tile, preferred_element_type=f32
            ) * pattern[t, NEAR_REACH - gap]
        if a in own:
            t = a - NEAR_REACH
            near[t] = near[t] + lax.dot_general(
                values[b], tile, (((1,), (1,)), ((), ())), preferred_element_type=f32
            ) * pattern[t, NEAR_REACH + gap]

    gathered = lax.all_gather(group_term, DEV, axis=0, tiled=False)
    own_coef = jnp.sum(gathered, axis=0).astype(jnp.bfloat16)
    group_index = lax.axis_index("group")
    group_total = lax.axis_size("group")
    late = 4
    for part, chunk in enumerate((jobs[:-late], jobs[-late:])):
        points_of, probes_of = wide_points, wide_probes
        if part:
            own_coef, points_of, probes_of = lax.optimization_barrier(
                (own_coef, points_of, probes_of)
            )
            group_coef = {
                shift: cyclic_from_behind(own_coef, "group", shift)
                for shift in range(1, group_total)
            }
        at = dict(zip(range(wide), [points_of[i] for i in range(wide)]))
        values = dict(zip(range(wide), [probes_of[i] for i in range(wide)]))
        for job in chunk:
            run_job(job, at, values)
    near = jnp.stack(near)

    own_skeleton = lax.dynamic_index_in_dim(group_skeleton, group_index, 0, keepdims=False)
    far_group = jnp.zeros((probe_count, skeleton), f32)
    for shift in range(1, group_total):
        other = (group_index - shift) % group_total
        other_skeleton = lax.dynamic_index_in_dim(group_skeleton, other, 0, keepdims=False)
        kernel_tile = matern(other_skeleton, own_skeleton, signal_variance)
        far_group = far_group + jnp.dot(group_coef[shift], kernel_tile, preferred_element_type=f32)
    group_local = far_group.astype(jnp.bfloat16)

    own_node = lax.dynamic_index_in_dim(node_skeleton, node_index, 0, keepdims=False)
    far_node = jnp.zeros((probe_count, skeleton), f32)
    for offset in range(-COUPLE_REACH, COUPLE_REACH + 1):
        if abs(offset) < 2:
            continue
        partner = node_index + offset
        usable = (
            (partner >= 0) & (partner < node_total) & (node_coupling[0, offset + COUPLE_REACH] > 0)
        )
        clamped = jnp.clip(partner, 0, node_total - 1)
        partner_points = lax.dynamic_index_in_dim(node_skeleton, clamped, 0, keepdims=False)
        kernel_tile = matern(partner_points, own_node, signal_variance)
        contribution = jnp.dot(relayed[offset], kernel_tile, preferred_element_type=f32)
        far_node = far_node + jnp.where(usable, contribution, f32(0.0))

    pushed = lax.dot_general(
        group_local, group_transfer[0], (((1,), (1,)), ((), ())), preferred_element_type=f32
    )
    node_local = (pushed + far_node).astype(jnp.bfloat16)
    spread = lax.dot_general(
        node_local, transfer_flat, (((1,), (1,)), ((), ())), preferred_element_type=f32
    )
    leaf_local = (
        spread.reshape(probe_count, leaf_count, skeleton).transpose(1, 0, 2).astype(jnp.bfloat16)
    )
    far_leaf = lax.dot_general(
        leaf_local, leaf_basis, (((2,), (2,)), ((0,), (0,))), preferred_element_type=f32
    )
    result = (far_leaf + near + noise_variance * ordered.astype(f32)).astype(jnp.bfloat16)
    restored = [
        lax.dot_general(
            result[i], hots[i], (((1,), (1,)), ((), ())), preferred_element_type=f32
        ).astype(jnp.bfloat16)
        for i in range(leaf_count)
    ]
    return jnp.stack(restored)


def solution(mesh):
    finer = Mesh(mesh.devices.reshape(mesh.shape["group"], 4, 16), ("group", "dev_0", "dev_1"))
    return jax.shard_map(
        on_device,
        mesh=finer,
        in_specs=(
            P(GROUP_DEV, None, None),
            P(GROUP_DEV, None, None),
            P(GROUP_DEV, None),
            P(GROUP_DEV, None, None),
            P(GROUP_DEV, None, None, None),
            P(GROUP_DEV, None, None),
            P("group", None, None),
            P(),
            P(GROUP_DEV, None),
            P(GROUP_DEV, None),
            P(),
            P(),
        ),
        out_specs=P(GROUP_DEV, None, None),
        check_vma=False,
    )
```

```python
import jax
import jax.numpy as jnp
from jax import lax
from jax.sharding import Mesh
from jax.sharding import PartitionSpec as P

NEAR_REACH = 2
COUPLE_REACH = 4
GROUP_DEV = ("group", "dev_0", "dev_1")
DEV = ("dev_0", "dev_1")


ROOT_THREE = 1.7320508075688772
LENGTH_SCALE = 0.5


def with_halo(value, axis, width):
    peers, length = (lax.axis_size(axis), value.shape[0])
    up = [(i, i + 1) for i in range(peers - 1)]
    last = value[length - width :]
    leading = value[:width]
    low = lax.ppermute(last, axis, up)
    high = lax.ppermute(leading, axis, [(b, a) for a, b in up])
    return jnp.concatenate([low, value, high], axis=0)


def from_behind(block, axis, distance):
    devices = range(lax.axis_size(axis))
    route = [(i - distance, i) for i in devices if i - distance in devices]
    return lax.ppermute(block, axis, route)


def tree_sum(value, axis):
    peers = lax.axis_size(axis)
    step = 1
    while step < peers:
        value = value + lax.ppermute(value, axis, [(i, i ^ step) for i in range(peers)])
        step *= 2
    return value


def partner_sets(part):
    if part == "dev_0":
        peers = lax.axis_size("dev_0")
        return [("dev_0", [(i, (i + s) % peers) for i in range(peers)]) for s in range(1, peers)]
    peers = lax.axis_size("dev_1")
    block = 4
    if part == "dev_1_low":
        move = lambda i, s: (i // block) * block + (i % block + s) % block
    else:
        move = lambda i, s: (i + s * block) % peers
    return [("dev_1", [(i, move(i, s)) for i in range(peers)]) for s in range(1, block)]


def cyclic_from_behind(block, axis, distance):
    peers = lax.axis_size(axis)
    return lax.ppermute(block, axis, [(i, (i + distance) % peers) for i in range(peers)])


def matern(source, target, amplitude):
    square = (source[0][:, None] - target[0][None, :]) ** 2
    square = square + (source[1][:, None] - target[1][None, :]) ** 2
    square = square + (source[2][:, None] - target[2][None, :]) ** 2
    scaled = jnp.sqrt(square) * (ROOT_THREE / LENGTH_SCALE)
    return (amplitude * (1.0 + scaled) * jnp.exp(-scaled)).astype(jnp.bfloat16)


def one_hot(ordering, size):
    rows = lax.broadcasted_iota(jnp.int32, (size, size), 0)
    return (rows == ordering[None, :]).astype(jnp.bfloat16)


def on_device(
    probes,
    points,
    leaf_order,
    leaf_basis,
    node_transfer,
    group_transfer,
    node_skeleton,
    group_skeleton,
    near_pattern,
    node_coupling,
    signal_variance,
    noise_variance,
):
    leaf_count, probe_count, leaf_size = probes.shape
    skeleton = leaf_basis.shape[2]
    f32 = jnp.float32

    hots = [one_hot(leaf_order[i], leaf_size) for i in range(leaf_count)]
    ordered = jnp.stack(
        [
            jnp.dot(probes[i], hots[i], preferred_element_type=f32).astype(jnp.bfloat16)
            for i in range(leaf_count)
        ]
    )

    leaf_coef = lax.dot_general(
        ordered, leaf_basis, (((2,), (1,)), ((0,), (0,))), preferred_element_type=f32
    ).astype(jnp.bfloat16)
    stacked = leaf_coef.transpose(1, 0, 2).reshape(probe_count, leaf_count * skeleton)
    transfer_flat = node_transfer[0].reshape(leaf_count * skeleton, skeleton)
    node_coef = jnp.dot(stacked, transfer_flat, preferred_element_type=f32).astype(jnp.bfloat16)
    group_term = jnp.dot(node_coef, group_transfer[0], preferred_element_type=f32)
    node_index = lax.axis_index(DEV)
    node_total = lax.axis_size(DEV)
    relayed = {}
    for offset in range(-COUPLE_REACH, COUPLE_REACH + 1):
        if abs(offset) < 2:
            continue
        relayed[offset] = from_behind(node_coef, DEV, -offset)

    wide_probes = with_halo(ordered, GROUP_DEV, NEAR_REACH)
    wide_points = with_halo(points, GROUP_DEV, NEAR_REACH)
    wide = leaf_count + 2 * NEAR_REACH
    own = range(NEAR_REACH, NEAR_REACH + leaf_count)
    pattern = near_pattern.astype(f32)
    jobs = [(b, b) for b in own]
    cross = []
    for gap in range(1, NEAR_REACH + 1):
        for a in range(wide - gap):
            b = a + gap
            if a in own and b in own:
                jobs.append((a, b))
            elif a in own or b in own:
                cross.append((a, b))
    jobs += cross
    near = [jnp.zeros((probe_count, leaf_size), f32) for _ in range(leaf_count)]

    def run_job(job, at, values):
        a, b = job
        tile = matern(at[a], at[b], signal_variance)
        if a == b:
            t = b - NEAR_REACH
            near[t] = near[t] + jnp.dot(values[b], tile, preferred_element_type=f32) * pattern[
                t, NEAR_REACH
            ]
            return
        gap = b - a
        if a in own and b in own:
            tile = lax.optimization_barrier(tile)
        if b in own:
            t = b - NEAR_REACH
            near[t] = near[t] + jnp.dot(
                values[a], tile, preferred_element_type=f32
            ) * pattern[t, NEAR_REACH - gap]
        if a in own:
            t = a - NEAR_REACH
            near[t] = near[t] + lax.dot_general(
                values[b], tile, (((1,), (1,)), ((), ())), preferred_element_type=f32
            ) * pattern[t, NEAR_REACH + gap]

    rounds = ["dev_0", "dev_1_low", "dev_1_high"]
    steps = len(rounds) + 1
    running = group_term
    group_index = lax.axis_index("group")
    group_total = lax.axis_size("group")
    for step in range(steps):
        chunk = jobs[step * len(jobs) // steps : (step + 1) * len(jobs) // steps]
        if any(job in cross for job in chunk):
            running, at, values = lax.optimization_barrier((running, wide_points, wide_probes))
        else:
            running, at, values = lax.optimization_barrier((running, points, ordered))
            at = {b: at[b - NEAR_REACH] for b in own}
            values = {b: values[b - NEAR_REACH] for b in own}
        if step < len(rounds):
            received = [
                lax.ppermute(running, axis, pairs) for axis, pairs in partner_sets(rounds[step])
            ]
        else:
            own_coef = running.astype(jnp.bfloat16)
            group_coef = {
                shift: cyclic_from_behind(own_coef, "group", shift)
                for shift in range(1, group_total)
            }
        for job in chunk:
            run_job(job, at, values)
        if step < len(rounds):
            running = (running + received[1]) + (received[0] + received[2])
    near = jnp.stack(near)

    own_skeleton = lax.dynamic_index_in_dim(group_skeleton, group_index, 0, keepdims=False)
    far_group = jnp.zeros((probe_count, skeleton), f32)
    for shift in range(1, group_total):
        other = (group_index - shift) % group_total
        other_skeleton = lax.dynamic_index_in_dim(group_skeleton, other, 0, keepdims=False)
        kernel_tile = matern(other_skeleton, own_skeleton, signal_variance)
        far_group = far_group + jnp.dot(group_coef[shift], kernel_tile, preferred_element_type=f32)
    group_local = far_group.astype(jnp.bfloat16)

    own_node = lax.dynamic_index_in_dim(node_skeleton, node_index, 0, keepdims=False)
    far_node = jnp.zeros((probe_count, skeleton), f32)
    for offset in range(-COUPLE_REACH, COUPLE_REACH + 1):
        if abs(offset) < 2:
            continue
        partner = node_index + offset
        usable = (
            (partner >= 0) & (partner < node_total) & (node_coupling[0, offset + COUPLE_REACH] > 0)
        )
        clamped = jnp.clip(partner, 0, node_total - 1)
        partner_points = lax.dynamic_index_in_dim(node_skeleton, clamped, 0, keepdims=False)
        kernel_tile = matern(partner_points, own_node, signal_variance)
        contribution = jnp.dot(relayed[offset], kernel_tile, preferred_element_type=f32)
        far_node = far_node + jnp.where(usable, contribution, f32(0.0))

    pushed = lax.dot_general(
        group_local, group_transfer[0], (((1,), (1,)), ((), ())), preferred_element_type=f32
    )
    node_local = (pushed + far_node).astype(jnp.bfloat16)
    spread = lax.dot_general(
        node_local, transfer_flat, (((1,), (1,)), ((), ())), preferred_element_type=f32
    )
    leaf_local = (
        spread.reshape(probe_count, leaf_count, skeleton).transpose(1, 0, 2).astype(jnp.bfloat16)
    )
    far_leaf = lax.dot_general(
        leaf_local, leaf_basis, (((2,), (2,)), ((0,), (0,))), preferred_element_type=f32
    )
    result = (far_leaf + near + noise_variance * ordered.astype(f32)).astype(jnp.bfloat16)
    restored = [
        lax.dot_general(
            result[i], hots[i], (((1,), (1,)), ((), ())), preferred_element_type=f32
        ).astype(jnp.bfloat16)
        for i in range(leaf_count)
    ]
    return jnp.stack(restored)


def solution(mesh):
    finer = Mesh(mesh.devices.reshape(mesh.shape["group"], 4, 16), ("group", "dev_0", "dev_1"))
    return jax.shard_map(
        on_device,
        mesh=finer,
        in_specs=(
            P(GROUP_DEV, None, None),
            P(GROUP_DEV, None, None),
            P(GROUP_DEV, None),
            P(GROUP_DEV, None, None),
            P(GROUP_DEV, None, None, None),
            P(GROUP_DEV, None, None),
            P("group", None, None),
            P(),
            P(GROUP_DEV, None),
            P(GROUP_DEV, None),
            P(),
            P(),
        ),
        out_specs=P(GROUP_DEV, None, None),
        check_vma=False,
    )
```

```python
import jax
import jax.numpy as jnp
from jax import lax
from jax.sharding import Mesh
from jax.sharding import PartitionSpec as P

NEAR_REACH = 2
COUPLE_REACH = 4
GROUP_DEV = ("group", "dev_0", "dev_1", "dev_2")
DEV = ("dev_0", "dev_1", "dev_2")


ROOT_THREE = 1.7320508075688772
LENGTH_SCALE = 0.5


def with_halo(value, axis, width):
    peers, length = (lax.axis_size(axis), value.shape[0])
    up = [(i, i + 1) for i in range(peers - 1)]
    last = value[length - width :]
    leading = value[:width]
    low = lax.ppermute(last, axis, up)
    high = lax.ppermute(leading, axis, [(b, a) for a, b in up])
    return jnp.concatenate([low, value, high], axis=0)


def from_behind(block, axis, distance):
    devices = range(lax.axis_size(axis))
    route = [(i - distance, i) for i in devices if i - distance in devices]
    return lax.ppermute(block, axis, route)


def tree_sum(value, axis):
    peers = lax.axis_size(axis)
    step = 1
    while step < peers:
        value = value + lax.ppermute(value, axis, [(i, i ^ step) for i in range(peers)])
        step *= 2
    return value


def from_everyone(value, axis):
    peers = lax.axis_size(axis)
    return lax.all_to_all(
        jnp.broadcast_to(value[None], (peers, *value.shape)), axis, 0, 0, tiled=True
    )


def cyclic_from_behind(block, axis, distance):
    peers = lax.axis_size(axis)
    return lax.ppermute(block, axis, [(i, (i + distance) % peers) for i in range(peers)])


def matern(source, target, amplitude):
    square = (source[0][:, None] - target[0][None, :]) ** 2
    square = square + (source[1][:, None] - target[1][None, :]) ** 2
    square = square + (source[2][:, None] - target[2][None, :]) ** 2
    scaled = jnp.sqrt(square) * (ROOT_THREE / LENGTH_SCALE)
    return (amplitude * (1.0 + scaled) * jnp.exp(-scaled)).astype(jnp.bfloat16)


def one_hot(ordering, size):
    rows = lax.broadcasted_iota(jnp.int32, (size, size), 0)
    return (rows == ordering[None, :]).astype(jnp.bfloat16)


def on_device(
    probes,
    points,
    leaf_order,
    leaf_basis,
    node_transfer,
    group_transfer,
    node_skeleton,
    group_skeleton,
    near_pattern,
    node_coupling,
    signal_variance,
    noise_variance,
):
    leaf_count, probe_count, leaf_size = probes.shape
    skeleton = leaf_basis.shape[2]
    f32 = jnp.float32

    hots = [one_hot(leaf_order[i], leaf_size) for i in range(leaf_count)]
    ordered = jnp.stack(
        [
            jnp.dot(probes[i], hots[i], preferred_element_type=f32).astype(jnp.bfloat16)
            for i in range(leaf_count)
        ]
    )

    leaf_coef = lax.dot_general(
        ordered, leaf_basis, (((2,), (1,)), ((0,), (0,))), preferred_element_type=f32
    ).astype(jnp.bfloat16)
    stacked = leaf_coef.transpose(1, 0, 2).reshape(probe_count, leaf_count * skeleton)
    transfer_flat = node_transfer[0].reshape(leaf_count * skeleton, skeleton)
    node_coef = jnp.dot(stacked, transfer_flat, preferred_element_type=f32).astype(jnp.bfloat16)
    group_term = jnp.dot(node_coef, group_transfer[0], preferred_element_type=f32)
    node_index = lax.axis_index(DEV)
    node_total = lax.axis_size(DEV)
    relayed = {}
    for offset in range(-COUPLE_REACH, COUPLE_REACH + 1):
        if abs(offset) < 2:
            continue
        relayed[offset] = from_behind(node_coef, DEV, -offset)

    wide_probes = with_halo(ordered, GROUP_DEV, NEAR_REACH)
    wide_points = with_halo(points, GROUP_DEV, NEAR_REACH)
    wide = leaf_count + 2 * NEAR_REACH
    own = range(NEAR_REACH, NEAR_REACH + leaf_count)
    pattern = near_pattern.astype(f32)
    jobs = [(b, b) for b in own]
    cross = []
    for gap in range(1, NEAR_REACH + 1):
        for a in range(wide - gap):
            b = a + gap
            if a in own and b in own:
                jobs.append((a, b))
            elif a in own or b in own:
                cross.append((a, b))
    jobs += cross
    near = [jnp.zeros((probe_count, leaf_size), f32) for _ in range(leaf_count)]

    def run_job(job, at, values):
        a, b = job
        tile = matern(at[a], at[b], signal_variance)
        if a == b:
            t = b - NEAR_REACH
            near[t] = near[t] + jnp.dot(values[b], tile, preferred_element_type=f32) * pattern[
                t, NEAR_REACH
            ]
            return
        gap = b - a
        if a in own and b in own:
            tile = lax.optimization_barrier(tile)
        if b in own:
            t = b - NEAR_REACH
            near[t] = near[t] + jnp.dot(
                values[a], tile, preferred_element_type=f32
            ) * pattern[t, NEAR_REACH - gap]
        if a in own:
            t = a - NEAR_REACH
            near[t] = near[t] + lax.dot_general(
                values[b], tile, (((1,), (1,)), ((), ())), preferred_element_type=f32
            ) * pattern[t, NEAR_REACH + gap]

    rounds = ["dev_0", "dev_2", "dev_1"]
    steps = len(rounds) + 1
    running = group_term
    group_index = lax.axis_index("group")
    group_total = lax.axis_size("group")
    for step in range(steps):
        chunk = jobs[step * len(jobs) // steps : (step + 1) * len(jobs) // steps]
        if any(job in cross for job in chunk):
            running, at, values = lax.optimization_barrier((running, wide_points, wide_probes))
        else:
            running, at, values = lax.optimization_barrier((running, points, ordered))
            at = {b: at[b - NEAR_REACH] for b in own}
            values = {b: values[b - NEAR_REACH] for b in own}
        if step < len(rounds):
            received = from_everyone(running, rounds[step])
        else:
            own_coef = running.astype(jnp.bfloat16)
            group_coef = from_everyone(own_coef, "group")
        for job in chunk:
            run_job(job, at, values)
        if step < len(rounds):
            running = jnp.sum(received, axis=0)
    near = jnp.stack(near)

    own_skeleton = lax.dynamic_index_in_dim(group_skeleton, group_index, 0, keepdims=False)
    far_group = jnp.zeros((probe_count, skeleton), f32)
    for other in range(group_total):
        kernel_tile = matern(group_skeleton[other], own_skeleton, signal_variance)
        contribution = jnp.dot(group_coef[other], kernel_tile, preferred_element_type=f32)
        far_group = far_group + jnp.where(other != group_index, contribution, f32(0.0))
    group_local = far_group.astype(jnp.bfloat16)

    own_node = lax.dynamic_index_in_dim(node_skeleton, node_index, 0, keepdims=False)
    far_node = jnp.zeros((probe_count, skeleton), f32)
    for offset in range(-COUPLE_REACH, COUPLE_REACH + 1):
        if abs(offset) < 2:
            continue
        partner = node_index + offset
        usable = (
            (partner >= 0) & (partner < node_total) & (node_coupling[0, offset + COUPLE_REACH] > 0)
        )
        clamped = jnp.clip(partner, 0, node_total - 1)
        partner_points = lax.dynamic_index_in_dim(node_skeleton, clamped, 0, keepdims=False)
        kernel_tile = matern(partner_points, own_node, signal_variance)
        contribution = jnp.dot(relayed[offset], kernel_tile, preferred_element_type=f32)
        far_node = far_node + jnp.where(usable, contribution, f32(0.0))

    pushed = lax.dot_general(
        group_local, group_transfer[0], (((1,), (1,)), ((), ())), preferred_element_type=f32
    )
    node_local = (pushed + far_node).astype(jnp.bfloat16)
    spread = lax.dot_general(
        node_local, transfer_flat, (((1,), (1,)), ((), ())), preferred_element_type=f32
    )
    leaf_local = (
        spread.reshape(probe_count, leaf_count, skeleton).transpose(1, 0, 2).astype(jnp.bfloat16)
    )
    far_leaf = lax.dot_general(
        leaf_local, leaf_basis, (((2,), (2,)), ((0,), (0,))), preferred_element_type=f32
    )
    result = (far_leaf + near + noise_variance * ordered.astype(f32)).astype(jnp.bfloat16)
    restored = [
        lax.dot_general(
            result[i], hots[i], (((1,), (1,)), ((), ())), preferred_element_type=f32
        ).astype(jnp.bfloat16)
        for i in range(leaf_count)
    ]
    return jnp.stack(restored)


def solution(mesh):
    finer = Mesh(mesh.devices.reshape(mesh.shape["group"], 4, 4, 4), GROUP_DEV)
    return jax.shard_map(
        on_device,
        mesh=finer,
        in_specs=(
            P(GROUP_DEV, None, None),
            P(GROUP_DEV, None, None),
            P(GROUP_DEV, None),
            P(GROUP_DEV, None, None),
            P(GROUP_DEV, None, None, None),
            P(GROUP_DEV, None, None),
            P("group", None, None),
            P(),
            P(GROUP_DEV, None),
            P(GROUP_DEV, None),
            P(),
            P(),
        ),
        out_specs=P(GROUP_DEV, None, None),
        check_vma=False,
    )
```

```python
import jax
import jax.numpy as jnp
from jax import lax
from jax.experimental import pallas as pl
from jax.experimental.pallas import tpu as pltpu
from jax.sharding import Mesh
from jax.sharding import PartitionSpec as P

NEAR_REACH = 2
COUPLE_REACH = 4
GROUP_DEV = ("group", "dev_0", "dev_1", "dev_2")
DEV = ("dev_0", "dev_1", "dev_2")


ROOT_THREE = 1.7320508075688772
LENGTH_SCALE = 0.5


def with_halo(value, axis, width):
    peers, length = (lax.axis_size(axis), value.shape[0])
    up = [(i, i + 1) for i in range(peers - 1)]
    last = value[length - width :]
    leading = value[:width]
    low = lax.ppermute(last, axis, up)
    high = lax.ppermute(leading, axis, [(b, a) for a, b in up])
    return jnp.concatenate([low, value, high], axis=0)


def from_behind(block, axis, distance):
    devices = range(lax.axis_size(axis))
    route = [(i - distance, i) for i in devices if i - distance in devices]
    return lax.ppermute(block, axis, route)


def from_everyone(value, axis):
    peers = lax.axis_size(axis)
    return lax.all_to_all(
        jnp.broadcast_to(value[None], (peers, *value.shape)), axis, 0, 0, tiled=True
    )


def matern(source, target, amplitude):
    square = (source[0][:, None] - target[0][None, :]) ** 2
    square = square + (source[1][:, None] - target[1][None, :]) ** 2
    square = square + (source[2][:, None] - target[2][None, :]) ** 2
    scaled = jnp.sqrt(square) * (ROOT_THREE / LENGTH_SCALE)
    return (amplitude * (1.0 + scaled) * jnp.exp(-scaled)).astype(jnp.bfloat16)


def near_kernel(pattern_ref, amp_ref, target_ref, source_ref, probes_ref, out_ref, tile_ref):
    t = pl.program_id(0)
    window = 2 * NEAR_REACH + 1
    size = target_ref.shape[-1]
    chunk = tile_ref.shape[0]
    rows = 16
    amp = amp_ref[0]
    tx = target_ref[0, 0:1, :]
    ty = target_ref[0, 1:2, :]
    tz = target_ref[0, 2:3, :]
    out_ref[0] = jnp.zeros(out_ref.shape[1:], jnp.float32)
    for o in range(window):
        s = t + o

        @pl.when(pattern_ref[t, o] != 0)
        def _():
            def body(c, carry):
                start = pl.multiple_of(c * chunk, chunk)
                for r in range(chunk // rows):
                    col = source_ref[s, pl.ds(start + r * rows, rows), :]
                    dx = col[:, 0:1] - tx
                    dy = col[:, 1:2] - ty
                    dz = col[:, 2:3] - tz
                    square = dx * dx
                    square = square + dy * dy
                    square = square + dz * dz
                    scaled = jnp.sqrt(square) * (ROOT_THREE / LENGTH_SCALE)
                    value = amp * (1.0 + scaled) * jnp.exp(-scaled)
                    tile_ref[r * rows : (r + 1) * rows, :] = value.astype(jnp.bfloat16)
                values = probes_ref[s, :, pl.ds(start, chunk)]
                out_ref[0] += jnp.dot(values, tile_ref[...], preferred_element_type=jnp.float32)
                return carry

            lax.fori_loop(0, size // chunk, body, 0)


def near_field(pattern, amplitude, targets, sources_t, wide_probes):
    leaves, _, size = targets.shape
    probe_count = wide_probes.shape[1]
    chunk = 128
    return pl.pallas_call(
        near_kernel,
        grid=(leaves,),
        in_specs=[
            pl.BlockSpec(memory_space=pltpu.SMEM),
            pl.BlockSpec(memory_space=pltpu.SMEM),
            pl.BlockSpec((1, 3, size), lambda t: (t, 0, 0)),
            pl.BlockSpec(sources_t.shape, lambda t: (0, 0, 0)),
            pl.BlockSpec(wide_probes.shape, lambda t: (0, 0, 0)),
        ],
        out_specs=pl.BlockSpec((1, probe_count, size), lambda t: (t, 0, 0)),
        out_shape=jax.ShapeDtypeStruct((leaves, probe_count, size), jnp.float32),
        scratch_shapes=[pltpu.VMEM((chunk, size), jnp.bfloat16)],
    )(pattern, amplitude.reshape(1), targets, sources_t, wide_probes)


def one_hot(ordering, size):
    rows = lax.broadcasted_iota(jnp.int32, (size, size), 0)
    return (rows == ordering[None, :]).astype(jnp.bfloat16)


def on_device(
    probes,
    points,
    leaf_order,
    leaf_basis,
    node_transfer,
    group_transfer,
    node_skeleton,
    group_skeleton,
    near_pattern,
    node_coupling,
    signal_variance,
    noise_variance,
):
    leaf_count, probe_count, leaf_size = probes.shape
    skeleton = leaf_basis.shape[2]
    f32 = jnp.float32

    hots = [one_hot(leaf_order[i], leaf_size) for i in range(leaf_count)]
    ordered = jnp.stack(
        [
            jnp.dot(probes[i], hots[i], preferred_element_type=f32).astype(jnp.bfloat16)
            for i in range(leaf_count)
        ]
    )

    leaf_coef = lax.dot_general(
        ordered, leaf_basis, (((2,), (1,)), ((0,), (0,))), preferred_element_type=f32
    ).astype(jnp.bfloat16)
    stacked = leaf_coef.transpose(1, 0, 2).reshape(probe_count, leaf_count * skeleton)
    transfer_flat = node_transfer[0].reshape(leaf_count * skeleton, skeleton)
    node_coef = jnp.dot(stacked, transfer_flat, preferred_element_type=f32).astype(jnp.bfloat16)
    group_term = jnp.dot(node_coef, group_transfer[0], preferred_element_type=f32)
    node_index = lax.axis_index(DEV)
    node_total = lax.axis_size(DEV)
    relayed = {}
    for offset in range(-COUPLE_REACH, COUPLE_REACH + 1):
        if abs(offset) < 2:
            continue
        relayed[offset] = from_behind(node_coef, DEV, -offset)

    wide_probes = with_halo(ordered, GROUP_DEV, NEAR_REACH)
    wide_points = with_halo(points, GROUP_DEV, NEAR_REACH)
    sources_t = jnp.transpose(wide_points, (0, 2, 1))
    window = 2 * NEAR_REACH + 1

    rounds = ["dev_0", "dev_2", "dev_1"]
    running = group_term
    group_index = lax.axis_index("group")
    group_total = lax.axis_size("group")
    parts = []
    for step in range(leaf_count):
        running, points_of, probes_of, sources_of = lax.optimization_barrier(
            (running, wide_points, wide_probes, sources_t)
        )
        if step < len(rounds):
            received = from_everyone(running, rounds[step])
        else:
            own_coef = running.astype(jnp.bfloat16)
            group_coef = from_everyone(own_coef, "group")
        parts.append(
            near_field(
                near_pattern[step : step + 1],
                signal_variance,
                points_of[step + NEAR_REACH : step + NEAR_REACH + 1],
                sources_of[step : step + window],
                probes_of[step : step + window],
            )
        )
        if step < len(rounds):
            running = jnp.sum(received, axis=0)
    near = jnp.concatenate(parts, axis=0)

    own_skeleton = lax.dynamic_index_in_dim(group_skeleton, group_index, 0, keepdims=False)
    far_group = jnp.zeros((probe_count, skeleton), f32)
    for other in range(group_total):
        kernel_tile = matern(group_skeleton[other], own_skeleton, signal_variance)
        contribution = jnp.dot(group_coef[other], kernel_tile, preferred_element_type=f32)
        far_group = far_group + jnp.where(other != group_index, contribution, f32(0.0))
    group_local = far_group.astype(jnp.bfloat16)

    own_node = lax.dynamic_index_in_dim(node_skeleton, node_index, 0, keepdims=False)
    far_node = jnp.zeros((probe_count, skeleton), f32)
    for offset in range(-COUPLE_REACH, COUPLE_REACH + 1):
        if abs(offset) < 2:
            continue
        partner = node_index + offset
        usable = (
            (partner >= 0) & (partner < node_total) & (node_coupling[0, offset + COUPLE_REACH] > 0)
        )
        clamped = jnp.clip(partner, 0, node_total - 1)
        partner_points = lax.dynamic_index_in_dim(node_skeleton, clamped, 0, keepdims=False)
        kernel_tile = matern(partner_points, own_node, signal_variance)
        contribution = jnp.dot(relayed[offset], kernel_tile, preferred_element_type=f32)
        far_node = far_node + jnp.where(usable, contribution, f32(0.0))

    pushed = lax.dot_general(
        group_local, group_transfer[0], (((1,), (1,)), ((), ())), preferred_element_type=f32
    )
    node_local = (pushed + far_node).astype(jnp.bfloat16)
    spread = lax.dot_general(
        node_local, transfer_flat, (((1,), (1,)), ((), ())), preferred_element_type=f32
    )
    leaf_local = (
        spread.reshape(probe_count, leaf_count, skeleton).transpose(1, 0, 2).astype(jnp.bfloat16)
    )
    far_leaf = lax.dot_general(
        leaf_local, leaf_basis, (((2,), (2,)), ((0,), (0,))), preferred_element_type=f32
    )
    result = (far_leaf + near + noise_variance * ordered.astype(f32)).astype(jnp.bfloat16)
    restored = [
        lax.dot_general(
            result[i], hots[i], (((1,), (1,)), ((), ())), preferred_element_type=f32
        ).astype(jnp.bfloat16)
        for i in range(leaf_count)
    ]
    return jnp.stack(restored)


def solution(mesh):
    finer = Mesh(mesh.devices.reshape(mesh.shape["group"], 4, 4, 4), GROUP_DEV)
    return jax.shard_map(
        on_device,
        mesh=finer,
        in_specs=(
            P(GROUP_DEV, None, None),
            P(GROUP_DEV, None, None),
            P(GROUP_DEV, None),
            P(GROUP_DEV, None, None),
            P(GROUP_DEV, None, None, None),
            P(GROUP_DEV, None, None),
            P("group", None, None),
            P(),
            P(GROUP_DEV, None),
            P(GROUP_DEV, None),
            P(),
            P(),
        ),
        out_specs=P(GROUP_DEV, None, None),
        check_vma=False,
    )
```

```python
import jax
import jax.numpy as jnp
from jax import lax
from jax.sharding import Mesh
from jax.sharding import PartitionSpec as P

NEAR_REACH = 2
COUPLE_REACH = 4
GROUP_DEV = ("group", "dev_0", "dev_1", "dev_2")
DEV = ("dev_0", "dev_1", "dev_2")


ROOT_THREE = 1.7320508075688772
LENGTH_SCALE = 0.5


def with_halo(value, axis, width):
    peers, length = (lax.axis_size(axis), value.shape[0])
    up = [(i, i + 1) for i in range(peers - 1)]
    last = value[length - width :]
    leading = value[:width]
    low = lax.ppermute(last, axis, up)
    high = lax.ppermute(leading, axis, [(b, a) for a, b in up])
    return low, high


def spread_out(low, value, high):
    pieces = [low[i] for i in range(low.shape[0])] + [value[i] for i in range(value.shape[0])]
    return dict(enumerate(pieces + [high[i] for i in range(high.shape[0])]))


def from_behind(block, axis, distance):
    devices = range(lax.axis_size(axis))
    route = [(i - distance, i) for i in devices if i - distance in devices]
    return lax.ppermute(block, axis, route)


def tree_sum(value, axis):
    peers = lax.axis_size(axis)
    step = 1
    while step < peers:
        value = value + lax.ppermute(value, axis, [(i, i ^ step) for i in range(peers)])
        step *= 2
    return value


def from_everyone(value, axis):
    peers = lax.axis_size(axis)
    return lax.all_to_all(
        jnp.broadcast_to(value[None], (peers, *value.shape)), axis, 0, 0, tiled=True
    )


def cyclic_from_behind(block, axis, distance):
    peers = lax.axis_size(axis)
    return lax.ppermute(block, axis, [(i, (i + distance) % peers) for i in range(peers)])


def matern(source, target, amplitude):
    square = (source[0][:, None] - target[0][None, :]) ** 2
    square = square + (source[1][:, None] - target[1][None, :]) ** 2
    square = square + (source[2][:, None] - target[2][None, :]) ** 2
    scaled = jnp.sqrt(square) * (ROOT_THREE / LENGTH_SCALE)
    return (amplitude * (1.0 + scaled) * jnp.exp(-scaled)).astype(jnp.bfloat16)


def one_hot(ordering, size):
    rows = lax.broadcasted_iota(jnp.int32, (size, size), 0)
    return (rows == ordering[None, :]).astype(jnp.bfloat16)


def on_device(
    probes,
    points,
    leaf_order,
    leaf_basis,
    node_transfer,
    group_transfer,
    node_skeleton,
    group_skeleton,
    near_pattern,
    node_coupling,
    signal_variance,
    noise_variance,
):
    leaf_count, probe_count, leaf_size = probes.shape
    skeleton = leaf_basis.shape[2]
    f32 = jnp.float32

    hots = [one_hot(leaf_order[i], leaf_size) for i in range(leaf_count)]
    ordered = jnp.stack(
        [
            jnp.dot(probes[i], hots[i], preferred_element_type=f32).astype(jnp.bfloat16)
            for i in range(leaf_count)
        ]
    )

    leaf_coef = lax.dot_general(
        ordered, leaf_basis, (((2,), (1,)), ((0,), (0,))), preferred_element_type=f32
    ).astype(jnp.bfloat16)
    stacked = leaf_coef.transpose(1, 0, 2).reshape(probe_count, leaf_count * skeleton)
    transfer_flat = node_transfer[0].reshape(leaf_count * skeleton, skeleton)
    node_coef = jnp.dot(stacked, transfer_flat, preferred_element_type=f32).astype(jnp.bfloat16)
    group_term = jnp.dot(node_coef, group_transfer[0], preferred_element_type=f32)
    node_index = lax.axis_index(DEV)
    node_total = lax.axis_size(DEV)
    relayed = {}
    for offset in range(-COUPLE_REACH, COUPLE_REACH + 1):
        if abs(offset) < 2:
            continue
        relayed[offset] = from_behind(node_coef, DEV, -offset)

    probes_halo = with_halo(ordered, GROUP_DEV, NEAR_REACH)
    points_halo = with_halo(points, GROUP_DEV, NEAR_REACH)
    wide = leaf_count + 2 * NEAR_REACH
    own = range(NEAR_REACH, NEAR_REACH + leaf_count)
    pattern = near_pattern.astype(f32)
    jobs = [(b, b) for b in own]
    cross = []
    for gap in range(1, NEAR_REACH + 1):
        for a in range(wide - gap):
            b = a + gap
            if a in own and b in own:
                jobs.append((a, b))
            elif a in own or b in own:
                cross.append((a, b))
    jobs += cross
    near = [jnp.zeros((probe_count, leaf_size), f32) for _ in range(leaf_count)]

    def run_job(job, at, values):
        a, b = job
        tile = matern(at[a], at[b], signal_variance)
        if a == b:
            t = b - NEAR_REACH
            near[t] = near[t] + jnp.dot(values[b], tile, preferred_element_type=f32) * pattern[
                t, NEAR_REACH
            ]
            return
        gap = b - a
        if a in own and b in own:
            tile = lax.optimization_barrier(tile)
        if b in own:
            t = b - NEAR_REACH
            near[t] = near[t] + jnp.dot(
                values[a], tile, preferred_element_type=f32
            ) * pattern[t, NEAR_REACH - gap]
        if a in own:
            t = a - NEAR_REACH
            near[t] = near[t] + lax.dot_general(
                values[b], tile, (((1,), (1,)), ((), ())), preferred_element_type=f32
            ) * pattern[t, NEAR_REACH + gap]

    rounds = ["dev_0", "dev_2", "dev_1"]
    steps = len(rounds) + 1
    running = group_term
    group_index = lax.axis_index("group")
    group_total = lax.axis_size("group")
    for step in range(steps):
        chunk = jobs[step * len(jobs) // steps : (step + 1) * len(jobs) // steps]
        if any(job in cross for job in chunk):
            running, points_of, probes_of, points_halo, probes_halo = lax.optimization_barrier(
                (running, points, ordered, points_halo, probes_halo)
            )
            at = spread_out(points_halo[0], points_of, points_halo[1])
            values = spread_out(probes_halo[0], probes_of, probes_halo[1])
        else:
            running, at, values = lax.optimization_barrier((running, points, ordered))
            at = {b: at[b - NEAR_REACH] for b in own}
            values = {b: values[b - NEAR_REACH] for b in own}
        if step < len(rounds):
            received = from_everyone(running, rounds[step])
        else:
            own_coef = running.astype(jnp.bfloat16)
            group_coef = from_everyone(own_coef, "group")
        for job in chunk:
            run_job(job, at, values)
        if step < len(rounds):
            running = jnp.sum(received, axis=0)
    near = jnp.stack(near)

    own_skeleton = lax.dynamic_index_in_dim(group_skeleton, group_index, 0, keepdims=False)
    group_tiles = matern(
        group_skeleton.transpose(1, 0, 2).reshape(3, group_total * skeleton),
        own_skeleton,
        signal_variance,
    )
    others = lax.broadcasted_iota(jnp.int32, (group_total, 1, 1), 0) != group_index
    group_stack = jnp.where(others, group_coef, jnp.zeros_like(group_coef))
    group_stack = group_stack.transpose(1, 0, 2).reshape(probe_count, group_total * skeleton)
    far_group = jnp.dot(group_stack, group_tiles, preferred_element_type=f32)
    group_local = far_group.astype(jnp.bfloat16)

    own_node = lax.dynamic_index_in_dim(node_skeleton, node_index, 0, keepdims=False)
    partner_points, partner_coefs = [], []
    for offset in range(-COUPLE_REACH, COUPLE_REACH + 1):
        if abs(offset) < 2:
            continue
        partner = node_index + offset
        usable = (
            (partner >= 0) & (partner < node_total) & (node_coupling[0, offset + COUPLE_REACH] > 0)
        )
        clamped = jnp.clip(partner, 0, node_total - 1)
        partner_points.append(lax.dynamic_index_in_dim(node_skeleton, clamped, 0, keepdims=False))
        partner_coefs.append(jnp.where(usable, relayed[offset], jnp.zeros_like(relayed[offset])))
    couple_tiles = matern(jnp.concatenate(partner_points, axis=1), own_node, signal_variance)
    far_node = jnp.dot(
        jnp.concatenate(partner_coefs, axis=1), couple_tiles, preferred_element_type=f32
    )

    pushed = lax.dot_general(
        group_local, group_transfer[0], (((1,), (1,)), ((), ())), preferred_element_type=f32
    )
    node_local = (pushed + far_node).astype(jnp.bfloat16)
    spread = lax.dot_general(
        node_local, transfer_flat, (((1,), (1,)), ((), ())), preferred_element_type=f32
    )
    leaf_local = (
        spread.reshape(probe_count, leaf_count, skeleton).transpose(1, 0, 2).astype(jnp.bfloat16)
    )
    far_leaf = lax.dot_general(
        leaf_local, leaf_basis, (((2,), (2,)), ((0,), (0,))), preferred_element_type=f32
    )
    result = (far_leaf + near + noise_variance * ordered.astype(f32)).astype(jnp.bfloat16)
    restored = [
        lax.dot_general(
            result[i], hots[i], (((1,), (1,)), ((), ())), preferred_element_type=f32
        ).astype(jnp.bfloat16)
        for i in range(leaf_count)
    ]
    return jnp.stack(restored)


def solution(mesh):
    finer = Mesh(mesh.devices.reshape(mesh.shape["group"], 4, 4, 4), GROUP_DEV)
    return jax.shard_map(
        on_device,
        mesh=finer,
        in_specs=(
            P(GROUP_DEV, None, None),
            P(GROUP_DEV, None, None),
            P(GROUP_DEV, None),
            P(GROUP_DEV, None, None),
            P(GROUP_DEV, None, None, None),
            P(GROUP_DEV, None, None),
            P("group", None, None),
            P(),
            P(GROUP_DEV, None),
            P(GROUP_DEV, None),
            P(),
            P(),
        ),
        out_specs=P(GROUP_DEV, None, None),
        check_vma=False,
    )
```

```python
import jax
import jax.numpy as jnp
from jax import lax
from jax.sharding import Mesh
from jax.sharding import PartitionSpec as P

NEAR_REACH = 2
COUPLE_REACH = 4
GROUP_DEV = ("group", "dev_0", "dev_1", "dev_2")
DEV = ("dev_0", "dev_1", "dev_2")


ROOT_THREE = 1.7320508075688772
LENGTH_SCALE = 0.5


def with_halo(value, axis, width):
    peers, length = (lax.axis_size(axis), value.shape[0])
    up = [(i, i + 1) for i in range(peers - 1)]
    last = value[length - width :]
    leading = value[:width]
    low = lax.ppermute(last, axis, up)
    high = lax.ppermute(leading, axis, [(b, a) for a, b in up])
    return low, high


def spread_out(low, value, high):
    pieces = [low[i] for i in range(low.shape[0])] + [value[i] for i in range(value.shape[0])]
    return dict(enumerate(pieces + [high[i] for i in range(high.shape[0])]))


def from_behind(block, axis, distance):
    devices = range(lax.axis_size(axis))
    route = [(i - distance, i) for i in devices if i - distance in devices]
    return lax.ppermute(block, axis, route)


def tree_sum(value, axis):
    peers = lax.axis_size(axis)
    step = 1
    while step < peers:
        value = value + lax.ppermute(value, axis, [(i, i ^ step) for i in range(peers)])
        step *= 2
    return value


def from_everyone(value, axis):
    peers = lax.axis_size(axis)
    return lax.all_to_all(
        jnp.broadcast_to(value[None], (peers, *value.shape)), axis, 0, 0, tiled=True
    )


def cyclic_from_behind(block, axis, distance):
    peers = lax.axis_size(axis)
    return lax.ppermute(block, axis, [(i, (i + distance) % peers) for i in range(peers)])


def matern(source, target, amplitude):
    square = (source[0][:, None] - target[0][None, :]) ** 2
    square = square + (source[1][:, None] - target[1][None, :]) ** 2
    square = square + (source[2][:, None] - target[2][None, :]) ** 2
    scaled = jnp.sqrt(square) * (ROOT_THREE / LENGTH_SCALE)
    return (amplitude * (1.0 + scaled) * jnp.exp(-scaled)).astype(jnp.bfloat16)


def one_hot(ordering, size):
    rows = lax.broadcasted_iota(jnp.int32, (size, size), 0)
    return (rows == ordering[None, :]).astype(jnp.bfloat16)


def on_device(
    probes,
    points,
    leaf_order,
    leaf_basis,
    node_transfer,
    group_transfer,
    node_skeleton,
    group_skeleton,
    near_pattern,
    node_coupling,
    signal_variance,
    noise_variance,
):
    leaf_count, probe_count, leaf_size = probes.shape
    skeleton = leaf_basis.shape[2]
    f32 = jnp.float32

    hots = [one_hot(leaf_order[i], leaf_size) for i in range(leaf_count)]
    ordered = jnp.stack(
        [
            jnp.dot(probes[i], hots[i], preferred_element_type=f32).astype(jnp.bfloat16)
            for i in range(leaf_count)
        ]
    )

    leaf_coef = lax.dot_general(
        ordered, leaf_basis, (((2,), (1,)), ((0,), (0,))), preferred_element_type=f32
    ).astype(jnp.bfloat16)
    stacked = leaf_coef.transpose(1, 0, 2).reshape(probe_count, leaf_count * skeleton)
    transfer_flat = node_transfer[0].reshape(leaf_count * skeleton, skeleton)
    node_coef = jnp.dot(stacked, transfer_flat, preferred_element_type=f32).astype(jnp.bfloat16)
    group_term = jnp.dot(node_coef, group_transfer[0], preferred_element_type=f32)
    node_index = lax.axis_index(DEV)
    node_total = lax.axis_size(DEV)

    probes_halo = with_halo(ordered, GROUP_DEV, NEAR_REACH)
    points_halo = with_halo(points, GROUP_DEV, NEAR_REACH)
    wide = leaf_count + 2 * NEAR_REACH
    own = range(NEAR_REACH, NEAR_REACH + leaf_count)
    pattern = near_pattern.astype(f32)
    jobs = [(b, b) for b in own]
    cross = []
    for gap in range(1, NEAR_REACH + 1):
        for a in range(wide - gap):
            b = a + gap
            if a in own and b in own:
                jobs.append((a, b))
            elif a in own or b in own:
                cross.append((a, b))
    jobs += cross
    near = [jnp.zeros((probe_count, leaf_size), f32) for _ in range(leaf_count)]

    def run_job(job, at, values):
        a, b = job
        tile = matern(at[a], at[b], signal_variance)
        if a == b:
            t = b - NEAR_REACH
            near[t] = near[t] + jnp.dot(values[b], tile, preferred_element_type=f32) * pattern[
                t, NEAR_REACH
            ]
            return
        gap = b - a
        if a in own and b in own:
            tile = lax.optimization_barrier(tile)
        if b in own:
            t = b - NEAR_REACH
            near[t] = near[t] + jnp.dot(
                values[a], tile, preferred_element_type=f32
            ) * pattern[t, NEAR_REACH - gap]
        if a in own:
            t = a - NEAR_REACH
            near[t] = near[t] + lax.dot_general(
                values[b], tile, (((1,), (1,)), ((), ())), preferred_element_type=f32
            ) * pattern[t, NEAR_REACH + gap]

    rounds = ["dev_2", "dev_1", "dev_0"]
    steps = len(rounds) + 1
    running = group_term
    extra = node_coef.astype(f32)[None]
    block = lax.axis_size("dev_2")
    row = block * lax.axis_size("dev_1")
    group_index = lax.axis_index("group")
    group_total = lax.axis_size("group")
    for step in range(steps):
        chunk = jobs[step * len(jobs) // steps : (step + 1) * len(jobs) // steps]
        if any(job in cross for job in chunk):
            running, extra, points_of, probes_of, points_halo, probes_halo = (
                lax.optimization_barrier(
                    (running, extra, points, ordered, points_halo, probes_halo)
                )
            )
            at = spread_out(points_halo[0], points_of, points_halo[1])
            values = spread_out(probes_halo[0], probes_of, probes_halo[1])
        else:
            running, extra, at, values = lax.optimization_barrier((running, extra, points, ordered))
            at = {b: at[b - NEAR_REACH] for b in own}
            values = {b: values[b - NEAR_REACH] for b in own}
        if step < len(rounds):
            received = from_everyone(jnp.concatenate([running[None], extra]), rounds[step])
        else:
            own_coef = running.astype(jnp.bfloat16)
            group_coef = from_everyone(own_coef, "group")
        for job in chunk:
            run_job(job, at, values)
        if step < len(rounds):
            running = jnp.sum(received[:, 0], axis=0)
            if step == 0:
                extra = received[:, 1]
            elif step == 1:
                row_coef = received[:, 1:].reshape(row, probe_count, skeleton)
                extra = jnp.concatenate([row_coef[:COUPLE_REACH], row_coef[row - COUPLE_REACH :]])
            else:
                ends_coef = received[:, 1:]
    near = jnp.stack(near)

    own_skeleton = lax.dynamic_index_in_dim(group_skeleton, group_index, 0, keepdims=False)
    group_tiles = matern(
        group_skeleton.transpose(1, 0, 2).reshape(3, group_total * skeleton),
        own_skeleton,
        signal_variance,
    )
    others = lax.broadcasted_iota(jnp.int32, (group_total, 1, 1), 0) != group_index
    group_stack = jnp.where(others, group_coef, jnp.zeros_like(group_coef))
    group_stack = group_stack.transpose(1, 0, 2).reshape(probe_count, group_total * skeleton)
    far_group = jnp.dot(group_stack, group_tiles, preferred_element_type=f32)
    group_local = far_group.astype(jnp.bfloat16)

    own_node = lax.dynamic_index_in_dim(node_skeleton, node_index, 0, keepdims=False)
    partner_points, partner_coefs = [], []
    for offset in range(-COUPLE_REACH, COUPLE_REACH + 1):
        if abs(offset) < 2:
            continue
        partner = node_index + offset
        usable = (
            (partner >= 0) & (partner < node_total) & (node_coupling[0, offset + COUPLE_REACH] > 0)
        )
        clamped = jnp.clip(partner, 0, node_total - 1)
        partner_points.append(lax.dynamic_index_in_dim(node_skeleton, clamped, 0, keepdims=False))
        along = node_index % row + offset
        line = node_index // row
        lines = lax.axis_size("dev_0")
        same = row_coef[jnp.clip(along, 0, row - 1)]
        below = ends_coef[jnp.clip(line - 1, 0, lines - 1), COUPLE_REACH + jnp.clip(along + COUPLE_REACH, 0, COUPLE_REACH - 1)]
        above = ends_coef[jnp.clip(line + 1, 0, lines - 1), jnp.clip(along - row, 0, COUPLE_REACH - 1)]
        coef = jnp.where(along < 0, below, jnp.where(along >= row, above, same))
        coef = coef.astype(jnp.bfloat16)
        partner_coefs.append(jnp.where(usable, coef, jnp.zeros_like(coef)))
    couple_tiles = matern(jnp.concatenate(partner_points, axis=1), own_node, signal_variance)
    far_node = jnp.dot(
        jnp.concatenate(partner_coefs, axis=1), couple_tiles, preferred_element_type=f32
    )

    pushed = lax.dot_general(
        group_local, group_transfer[0], (((1,), (1,)), ((), ())), preferred_element_type=f32
    )
    node_local = (pushed + far_node).astype(jnp.bfloat16)
    spread = lax.dot_general(
        node_local, transfer_flat, (((1,), (1,)), ((), ())), preferred_element_type=f32
    )
    leaf_local = (
        spread.reshape(probe_count, leaf_count, skeleton).transpose(1, 0, 2).astype(jnp.bfloat16)
    )
    far_leaf = lax.dot_general(
        leaf_local, leaf_basis, (((2,), (2,)), ((0,), (0,))), preferred_element_type=f32
    )
    result = (far_leaf + near + noise_variance * ordered.astype(f32)).astype(jnp.bfloat16)
    restored = [
        lax.dot_general(
            result[i], hots[i], (((1,), (1,)), ((), ())), preferred_element_type=f32
        ).astype(jnp.bfloat16)
        for i in range(leaf_count)
    ]
    return jnp.stack(restored)


def solution(mesh):
    finer = Mesh(mesh.devices.reshape(mesh.shape["group"], 4, 4, 4), GROUP_DEV)
    return jax.shard_map(
        on_device,
        mesh=finer,
        in_specs=(
            P(GROUP_DEV, None, None),
            P(GROUP_DEV, None, None),
            P(GROUP_DEV, None),
            P(GROUP_DEV, None, None),
            P(GROUP_DEV, None, None, None),
            P(GROUP_DEV, None, None),
            P("group", None, None),
            P(),
            P(GROUP_DEV, None),
            P(GROUP_DEV, None),
            P(),
            P(),
        ),
        out_specs=P(GROUP_DEV, None, None),
        check_vma=False,
    )
```

```python
import jax
import jax.numpy as jnp
from jax import lax
from jax.sharding import Mesh
from jax.sharding import PartitionSpec as P

NEAR_REACH = 2
COUPLE_REACH = 4
GROUP_DEV = ("group", "dev_0", "dev_1", "dev_2")
DEV = ("dev_0", "dev_1", "dev_2")


ROOT_THREE = 1.7320508075688772
LENGTH_SCALE = 0.5


def with_halo(value, axis, width):
    peers, length = (lax.axis_size(axis), value.shape[0])
    up = [(i, i + 1) for i in range(peers - 1)]
    last = value[length - width :]
    leading = value[:width]
    low = lax.ppermute(last, axis, up)
    high = lax.ppermute(leading, axis, [(b, a) for a, b in up])
    return low, high


def spread_out(low, value, high):
    pieces = [low[i] for i in range(low.shape[0])] + [value[i] for i in range(value.shape[0])]
    return dict(enumerate(pieces + [high[i] for i in range(high.shape[0])]))


def from_behind(block, axis, distance):
    devices = range(lax.axis_size(axis))
    route = [(i - distance, i) for i in devices if i - distance in devices]
    return lax.ppermute(block, axis, route)


def tree_sum(value, axis):
    peers = lax.axis_size(axis)
    step = 1
    while step < peers:
        value = value + lax.ppermute(value, axis, [(i, i ^ step) for i in range(peers)])
        step *= 2
    return value


def from_everyone(value, axis):
    peers = lax.axis_size(axis)
    return lax.all_to_all(
        jnp.broadcast_to(value[None], (peers, *value.shape)), axis, 0, 0, tiled=True
    )


def cyclic_from_behind(block, axis, distance):
    peers = lax.axis_size(axis)
    return lax.ppermute(block, axis, [(i, (i + distance) % peers) for i in range(peers)])


def matern(source, target, amplitude):
    square = (source[0][:, None] - target[0][None, :]) ** 2
    square = square + (source[1][:, None] - target[1][None, :]) ** 2
    square = square + (source[2][:, None] - target[2][None, :]) ** 2
    scaled = jnp.sqrt(square) * (ROOT_THREE / LENGTH_SCALE)
    return (amplitude * (1.0 + scaled) * jnp.exp(-scaled)).astype(jnp.bfloat16)


def one_hot(ordering, size):
    rows = lax.broadcasted_iota(jnp.int32, (size, size), 0)
    return (rows == ordering[None, :]).astype(jnp.bfloat16)


def on_device(
    probes,
    points,
    leaf_order,
    leaf_basis,
    node_transfer,
    group_transfer,
    node_skeleton,
    group_skeleton,
    near_pattern,
    node_coupling,
    signal_variance,
    noise_variance,
):
    leaf_count, probe_count, leaf_size = probes.shape
    skeleton = leaf_basis.shape[2]
    f32 = jnp.float32

    hots = [one_hot(leaf_order[i], leaf_size) for i in range(leaf_count)]
    ordered = jnp.stack(
        [
            jnp.dot(probes[i], hots[i], preferred_element_type=f32).astype(jnp.bfloat16)
            for i in range(leaf_count)
        ]
    )

    leaf_coef = lax.dot_general(
        ordered, leaf_basis, (((2,), (1,)), ((0,), (0,))), preferred_element_type=f32
    ).astype(jnp.bfloat16)
    stacked = leaf_coef.transpose(1, 0, 2).reshape(probe_count, leaf_count * skeleton)
    transfer_flat = node_transfer[0].reshape(leaf_count * skeleton, skeleton)
    node_coef = jnp.dot(stacked, transfer_flat, preferred_element_type=f32).astype(jnp.bfloat16)
    group_term = jnp.dot(node_coef, group_transfer[0], preferred_element_type=f32)
    node_index = lax.axis_index(DEV)
    node_total = lax.axis_size(DEV)

    probes_halo = with_halo(ordered, GROUP_DEV, NEAR_REACH)
    points_halo = with_halo(points, GROUP_DEV, NEAR_REACH)
    wide = leaf_count + 2 * NEAR_REACH
    own = range(NEAR_REACH, NEAR_REACH + leaf_count)
    pattern = near_pattern.astype(f32)
    jobs = [(b, b) for b in own]
    cross = []
    for gap in range(1, NEAR_REACH + 1):
        for a in range(wide - gap):
            b = a + gap
            if a in own and b in own:
                jobs.append((a, b))
            elif a in own or b in own:
                cross.append((a, b))
    jobs += cross
    near = [jnp.zeros((probe_count, leaf_size), f32) for _ in range(leaf_count)]

    def run_job(job, at, values):
        a, b = job
        tile = matern(at[a], at[b], signal_variance)
        if a == b:
            t = b - NEAR_REACH
            near[t] = near[t] + jnp.dot(values[b], tile, preferred_element_type=f32) * pattern[
                t, NEAR_REACH
            ]
            return
        gap = b - a
        if a in own and b in own:
            tile = lax.optimization_barrier(tile)
        if b in own:
            t = b - NEAR_REACH
            near[t] = near[t] + jnp.dot(
                values[a], tile, preferred_element_type=f32
            ) * pattern[t, NEAR_REACH - gap]
        if a in own:
            t = a - NEAR_REACH
            near[t] = near[t] + lax.dot_general(
                values[b], tile, (((1,), (1,)), ((), ())), preferred_element_type=f32
            ) * pattern[t, NEAR_REACH + gap]

    rounds = ["dev_1", "dev_2", "dev_0"]
    steps = len(rounds) + 1
    running = group_term
    extra = node_coef.astype(f32)[None]
    block = lax.axis_size("dev_2")
    row = block * lax.axis_size("dev_1")
    group_index = lax.axis_index("group")
    group_total = lax.axis_size("group")
    for step in range(steps):
        chunk = jobs[step * len(jobs) // steps : (step + 1) * len(jobs) // steps]
        if any(job in cross for job in chunk):
            running, extra, points_of, probes_of, points_halo, probes_halo = (
                lax.optimization_barrier(
                    (running, extra, points, ordered, points_halo, probes_halo)
                )
            )
            at = spread_out(points_halo[0], points_of, points_halo[1])
            values = spread_out(probes_halo[0], probes_of, probes_halo[1])
        else:
            running, extra, at, values = lax.optimization_barrier((running, extra, points, ordered))
            at = {b: at[b - NEAR_REACH] for b in own}
            values = {b: values[b - NEAR_REACH] for b in own}
        if step < len(rounds):
            received = from_everyone(jnp.concatenate([running[None], extra]), rounds[step])
        else:
            own_coef = running.astype(jnp.bfloat16)
            group_coef = from_everyone(own_coef, "group")
        for job in chunk:
            run_job(job, at, values)
        if step < len(rounds):
            running = jnp.sum(received[:, 0], axis=0)
            if step == 0:
                extra = received[:, 1]
            elif step == 1:
                row_coef = received[:, 1:].transpose(1, 0, 2, 3).reshape(row, probe_count, skeleton)
                extra = jnp.concatenate([row_coef[:COUPLE_REACH], row_coef[row - COUPLE_REACH :]])
            else:
                ends_coef = received[:, 1:]
    near = jnp.stack(near)

    own_skeleton = lax.dynamic_index_in_dim(group_skeleton, group_index, 0, keepdims=False)
    group_tiles = matern(
        group_skeleton.transpose(1, 0, 2).reshape(3, group_total * skeleton),
        own_skeleton,
        signal_variance,
    )
    others = lax.broadcasted_iota(jnp.int32, (group_total, 1, 1), 0) != group_index
    group_stack = jnp.where(others, group_coef, jnp.zeros_like(group_coef))
    group_stack = group_stack.transpose(1, 0, 2).reshape(probe_count, group_total * skeleton)
    far_group = jnp.dot(group_stack, group_tiles, preferred_element_type=f32)
    group_local = far_group.astype(jnp.bfloat16)

    own_node = lax.dynamic_index_in_dim(node_skeleton, node_index, 0, keepdims=False)
    partner_points, partner_coefs = [], []
    for offset in range(-COUPLE_REACH, COUPLE_REACH + 1):
        if abs(offset) < 2:
            continue
        partner = node_index + offset
        usable = (
            (partner >= 0) & (partner < node_total) & (node_coupling[0, offset + COUPLE_REACH] > 0)
        )
        clamped = jnp.clip(partner, 0, node_total - 1)
        partner_points.append(lax.dynamic_index_in_dim(node_skeleton, clamped, 0, keepdims=False))
        along = node_index % row + offset
        line = node_index // row
        lines = lax.axis_size("dev_0")
        same = row_coef[jnp.clip(along, 0, row - 1)]
        below = ends_coef[jnp.clip(line - 1, 0, lines - 1), COUPLE_REACH + jnp.clip(along + COUPLE_REACH, 0, COUPLE_REACH - 1)]
        above = ends_coef[jnp.clip(line + 1, 0, lines - 1), jnp.clip(along - row, 0, COUPLE_REACH - 1)]
        coef = jnp.where(along < 0, below, jnp.where(along >= row, above, same))
        coef = coef.astype(jnp.bfloat16)
        partner_coefs.append(jnp.where(usable, coef, jnp.zeros_like(coef)))
    couple_tiles = matern(jnp.concatenate(partner_points, axis=1), own_node, signal_variance)
    far_node = jnp.dot(
        jnp.concatenate(partner_coefs, axis=1), couple_tiles, preferred_element_type=f32
    )

    pushed = lax.dot_general(
        group_local, group_transfer[0], (((1,), (1,)), ((), ())), preferred_element_type=f32
    )
    node_local = (pushed + far_node).astype(jnp.bfloat16)
    spread = lax.dot_general(
        node_local, transfer_flat, (((1,), (1,)), ((), ())), preferred_element_type=f32
    )
    leaf_local = (
        spread.reshape(probe_count, leaf_count, skeleton).transpose(1, 0, 2).astype(jnp.bfloat16)
    )
    far_leaf = lax.dot_general(
        leaf_local, leaf_basis, (((2,), (2,)), ((0,), (0,))), preferred_element_type=f32
    )
    result = (far_leaf + near + noise_variance * ordered.astype(f32)).astype(jnp.bfloat16)
    restored = [
        lax.dot_general(
            result[i], hots[i], (((1,), (1,)), ((), ())), preferred_element_type=f32
        ).astype(jnp.bfloat16)
        for i in range(leaf_count)
    ]
    return jnp.stack(restored)


def solution(mesh):
    finer = Mesh(mesh.devices.reshape(mesh.shape["group"], 4, 4, 4), GROUP_DEV)
    return jax.shard_map(
        on_device,
        mesh=finer,
        in_specs=(
            P(GROUP_DEV, None, None),
            P(GROUP_DEV, None, None),
            P(GROUP_DEV, None),
            P(GROUP_DEV, None, None),
            P(GROUP_DEV, None, None, None),
            P(GROUP_DEV, None, None),
            P("group", None, None),
            P(),
            P(GROUP_DEV, None),
            P(GROUP_DEV, None),
            P(),
            P(),
        ),
        out_specs=P(GROUP_DEV, None, None),
        check_vma=False,
    )
```

```python
import jax
import jax.numpy as jnp
from jax import lax
from jax.sharding import Mesh
from jax.sharding import PartitionSpec as P

NEAR_REACH = 2
COUPLE_REACH = 4
GROUP_DEV = ("group", "dev_0", "dev_1", "dev_2")
DEV = ("dev_0", "dev_1", "dev_2")


ROOT_THREE = 1.7320508075688772
LENGTH_SCALE = 0.5


def with_halo(value, axis, width):
    peers, length = (lax.axis_size(axis), value.shape[0])
    up = [(i, i + 1) for i in range(peers - 1)]
    last = value[length - width :]
    leading = value[:width]
    low = lax.ppermute(last, axis, up)
    high = lax.ppermute(leading, axis, [(b, a) for a, b in up])
    return low, high


def spread_out(low, value, high):
    pieces = [low[i] for i in range(low.shape[0])] + [value[i] for i in range(value.shape[0])]
    return dict(enumerate(pieces + [high[i] for i in range(high.shape[0])]))


def from_behind(block, axis, distance):
    devices = range(lax.axis_size(axis))
    route = [(i - distance, i) for i in devices if i - distance in devices]
    return lax.ppermute(block, axis, route)


def tree_sum(value, axis):
    peers = lax.axis_size(axis)
    step = 1
    while step < peers:
        value = value + lax.ppermute(value, axis, [(i, i ^ step) for i in range(peers)])
        step *= 2
    return value


def from_everyone(value, axis):
    peers = lax.axis_size(axis)
    return lax.all_to_all(
        jnp.broadcast_to(value[None], (peers, *value.shape)), axis, 0, 0, tiled=True
    )


def cyclic_from_behind(block, axis, distance):
    peers = lax.axis_size(axis)
    return lax.ppermute(block, axis, [(i, (i + distance) % peers) for i in range(peers)])


def matern(source, target, amplitude):
    square = (source[0][:, None] - target[0][None, :]) ** 2
    square = square + (source[1][:, None] - target[1][None, :]) ** 2
    square = square + (source[2][:, None] - target[2][None, :]) ** 2
    scaled = jnp.sqrt(square) * (ROOT_THREE / LENGTH_SCALE)
    return (amplitude * (1.0 + scaled) * jnp.exp(-scaled)).astype(jnp.bfloat16)


def one_hot(ordering, size):
    rows = lax.broadcasted_iota(jnp.int32, (size, size), 0)
    return (rows == ordering[None, :]).astype(jnp.bfloat16)


def on_device(
    probes,
    points,
    leaf_order,
    leaf_basis,
    node_transfer,
    group_transfer,
    node_skeleton,
    group_skeleton,
    near_pattern,
    node_coupling,
    signal_variance,
    noise_variance,
):
    leaf_count, probe_count, leaf_size = probes.shape
    skeleton = leaf_basis.shape[2]
    f32 = jnp.float32

    hots = [one_hot(leaf_order[i], leaf_size) for i in range(leaf_count)]
    ordered = jnp.stack(
        [
            jnp.dot(probes[i], hots[i], preferred_element_type=f32).astype(jnp.bfloat16)
            for i in range(leaf_count)
        ]
    )

    leaf_coef = lax.dot_general(
        ordered, leaf_basis, (((2,), (1,)), ((0,), (0,))), preferred_element_type=f32
    ).astype(jnp.bfloat16)
    stacked = leaf_coef.transpose(1, 0, 2).reshape(probe_count, leaf_count * skeleton)
    transfer_flat = node_transfer[0].reshape(leaf_count * skeleton, skeleton)
    node_coef = jnp.dot(stacked, transfer_flat, preferred_element_type=f32).astype(jnp.bfloat16)
    group_term = jnp.dot(node_coef, group_transfer[0], preferred_element_type=f32)
    node_index = lax.axis_index(DEV)
    node_total = lax.axis_size(DEV)

    probes_halo = with_halo(ordered, GROUP_DEV, NEAR_REACH)
    points_halo = with_halo(points, GROUP_DEV, NEAR_REACH)
    wide = leaf_count + 2 * NEAR_REACH
    own = range(NEAR_REACH, NEAR_REACH + leaf_count)
    pattern = near_pattern.astype(f32)
    jobs = [(b, b) for b in own]
    cross = []
    for gap in range(1, NEAR_REACH + 1):
        for a in range(wide - gap):
            b = a + gap
            if a in own and b in own:
                jobs.append((a, b))
            elif a in own or b in own:
                cross.append((a, b))
    jobs += cross
    near = [jnp.zeros((probe_count, leaf_size), f32) for _ in range(leaf_count)]

    def run_job(job, at, values):
        a, b = job
        tile = matern(at[a], at[b], signal_variance)
        if a == b:
            t = b - NEAR_REACH
            near[t] = near[t] + jnp.dot(values[b], tile, preferred_element_type=f32) * pattern[
                t, NEAR_REACH
            ]
            return
        gap = b - a
        if a in own and b in own:
            tile = lax.optimization_barrier(tile)
        if b in own:
            t = b - NEAR_REACH
            near[t] = near[t] + jnp.dot(
                values[a], tile, preferred_element_type=f32
            ) * pattern[t, NEAR_REACH - gap]
        if a in own:
            t = a - NEAR_REACH
            near[t] = near[t] + lax.dot_general(
                values[b], tile, (((1,), (1,)), ((), ())), preferred_element_type=f32
            ) * pattern[t, NEAR_REACH + gap]

    rounds = ["dev_1", "dev_2", "dev_0"]
    steps = len(rounds) + 1
    running = group_term
    extra = node_coef.astype(f32)[None]
    block = lax.axis_size("dev_2")
    row = block * lax.axis_size("dev_1")
    group_index = lax.axis_index("group")
    group_total = lax.axis_size("group")
    for step in range(steps):
        chunk = jobs[step * len(jobs) // steps : (step + 1) * len(jobs) // steps]
        if any(job in cross for job in chunk):
            running, extra, points_of, probes_of, points_halo, probes_halo = (
                lax.optimization_barrier(
                    (running, extra, points, ordered, points_halo, probes_halo)
                )
            )
            at = spread_out(points_halo[0], points_of, points_halo[1])
            values = spread_out(probes_halo[0], probes_of, probes_halo[1])
        else:
            running, extra, at, values = lax.optimization_barrier((running, extra, points, ordered))
            at = {b: at[b - NEAR_REACH] for b in own}
            values = {b: values[b - NEAR_REACH] for b in own}
        if step < len(rounds):
            received = from_everyone(jnp.concatenate([running[None], extra]), rounds[step])
        else:
            own_coef = running.astype(jnp.bfloat16)
            group_coef = from_everyone(own_coef, "group")
        for job in chunk:
            run_job(job, at, values)
        if step < len(rounds):
            running = jnp.sum(received[:, 0], axis=0)
            if step == 0:
                extra = received[:, 1]
            elif step == 1:
                row_coef = received[:, 1:].transpose(1, 0, 2, 3).reshape(row, probe_count, skeleton)
                extra = jnp.concatenate([row_coef[:COUPLE_REACH], row_coef[row - COUPLE_REACH :]])
            else:
                ends_coef = received[:, 1:]
    near = jnp.stack(near)

    own_skeleton = lax.dynamic_index_in_dim(group_skeleton, group_index, 0, keepdims=False)
    group_tiles = matern(
        group_skeleton.transpose(1, 0, 2).reshape(3, group_total * skeleton),
        own_skeleton,
        signal_variance,
    )
    others = lax.broadcasted_iota(jnp.int32, (group_total, 1, 1), 0) != group_index
    group_stack = jnp.where(others, group_coef, jnp.zeros_like(group_coef))
    group_stack = group_stack.transpose(1, 0, 2).reshape(probe_count, group_total * skeleton)
    far_group = jnp.dot(group_stack, group_tiles, preferred_element_type=f32)
    group_local = far_group.astype(jnp.bfloat16)

    own_node = lax.dynamic_index_in_dim(node_skeleton, node_index, 0, keepdims=False)
    ends = ends_coef.shape[1]
    table = jnp.concatenate([row_coef, ends_coef.reshape(-1, probe_count, skeleton)])
    line = node_index // row
    lines = lax.axis_size("dev_0")
    partner_points, picks, usable = [], [], []
    for offset in range(-COUPLE_REACH, COUPLE_REACH + 1):
        if abs(offset) < 2:
            continue
        partner = node_index + offset
        usable.append(
            (partner >= 0) & (partner < node_total) & (node_coupling[0, offset + COUPLE_REACH] > 0)
        )
        clamped = jnp.clip(partner, 0, node_total - 1)
        partner_points.append(lax.dynamic_index_in_dim(node_skeleton, clamped, 0, keepdims=False))
        along = node_index % row + offset
        same = jnp.clip(along, 0, row - 1)
        below = row + jnp.clip(line - 1, 0, lines - 1) * ends + COUPLE_REACH
        below = below + jnp.clip(along + COUPLE_REACH, 0, COUPLE_REACH - 1)
        above = row + jnp.clip(line + 1, 0, lines - 1) * ends
        above = above + jnp.clip(along - row, 0, COUPLE_REACH - 1)
        picks.append(jnp.where(along < 0, below, jnp.where(along >= row, above, same)))
    picked = jnp.take(table, jnp.stack(picks), axis=0)
    picked = jnp.where(jnp.stack(usable)[:, None, None], picked, jnp.zeros_like(picked))
    picked = picked.astype(jnp.bfloat16).transpose(1, 0, 2).reshape(probe_count, -1)
    couple_tiles = matern(jnp.concatenate(partner_points, axis=1), own_node, signal_variance)
    far_node = jnp.dot(picked, couple_tiles, preferred_element_type=f32)

    pushed = lax.dot_general(
        group_local, group_transfer[0], (((1,), (1,)), ((), ())), preferred_element_type=f32
    )
    node_local = (pushed + far_node).astype(jnp.bfloat16)
    spread = lax.dot_general(
        node_local, transfer_flat, (((1,), (1,)), ((), ())), preferred_element_type=f32
    )
    leaf_local = (
        spread.reshape(probe_count, leaf_count, skeleton).transpose(1, 0, 2).astype(jnp.bfloat16)
    )
    far_leaf = lax.dot_general(
        leaf_local, leaf_basis, (((2,), (2,)), ((0,), (0,))), preferred_element_type=f32
    )
    result = (far_leaf + near + noise_variance * ordered.astype(f32)).astype(jnp.bfloat16)
    restored = [
        lax.dot_general(
            result[i], hots[i], (((1,), (1,)), ((), ())), preferred_element_type=f32
        ).astype(jnp.bfloat16)
        for i in range(leaf_count)
    ]
    return jnp.stack(restored)


def solution(mesh):
    finer = Mesh(mesh.devices.reshape(mesh.shape["group"], 4, 4, 4), GROUP_DEV)
    return jax.shard_map(
        on_device,
        mesh=finer,
        in_specs=(
            P(GROUP_DEV, None, None),
            P(GROUP_DEV, None, None),
            P(GROUP_DEV, None),
            P(GROUP_DEV, None, None),
            P(GROUP_DEV, None, None, None),
            P(GROUP_DEV, None, None),
            P("group", None, None),
            P(),
            P(GROUP_DEV, None),
            P(GROUP_DEV, None),
            P(),
            P(),
        ),
        out_specs=P(GROUP_DEV, None, None),
        check_vma=False,
    )
```

```python
import jax
import jax.numpy as jnp
from jax import lax
from jax.sharding import Mesh
from jax.sharding import PartitionSpec as P

NEAR_REACH = 2
COUPLE_REACH = 4
GROUP_DEV = ("group", "dev_0", "dev_1", "dev_2")
DEV = ("dev_0", "dev_1", "dev_2")


ROOT_THREE = 1.7320508075688772
LENGTH_SCALE = 0.5


def with_halo(value, axis, width):
    peers, length = (lax.axis_size(axis), value.shape[0])
    up = [(i, i + 1) for i in range(peers - 1)]
    leading = value[:width]
    return lax.ppermute(leading, axis, [(b, a) for a, b in up])


def spread_out(value, high, width):
    pieces = [value[i] for i in range(value.shape[0])] + [high[i] for i in range(high.shape[0])]
    return dict(enumerate(pieces, start=width))


def from_behind(block, axis, distance):
    devices = range(lax.axis_size(axis))
    route = [(i - distance, i) for i in devices if i - distance in devices]
    return lax.ppermute(block, axis, route)


def tree_sum(value, axis):
    peers = lax.axis_size(axis)
    step = 1
    while step < peers:
        value = value + lax.ppermute(value, axis, [(i, i ^ step) for i in range(peers)])
        step *= 2
    return value


def from_everyone(value, axis):
    peers = lax.axis_size(axis)
    return lax.all_to_all(
        jnp.broadcast_to(value[None], (peers, *value.shape)), axis, 0, 0, tiled=True
    )


def cyclic_from_behind(block, axis, distance):
    peers = lax.axis_size(axis)
    return lax.ppermute(block, axis, [(i, (i + distance) % peers) for i in range(peers)])


def matern(source, target, amplitude):
    square = (source[0][:, None] - target[0][None, :]) ** 2
    square = square + (source[1][:, None] - target[1][None, :]) ** 2
    square = square + (source[2][:, None] - target[2][None, :]) ** 2
    scaled = jnp.sqrt(square) * (ROOT_THREE / LENGTH_SCALE)
    return (amplitude * (1.0 + scaled) * jnp.exp(-scaled)).astype(jnp.bfloat16)


def one_hot(ordering, size):
    rows = lax.broadcasted_iota(jnp.int32, (size, size), 0)
    return (rows == ordering[None, :]).astype(jnp.bfloat16)


def on_device(
    probes,
    points,
    leaf_order,
    leaf_basis,
    node_transfer,
    group_transfer,
    node_skeleton,
    group_skeleton,
    near_pattern,
    node_coupling,
    signal_variance,
    noise_variance,
):
    leaf_count, probe_count, leaf_size = probes.shape
    skeleton = leaf_basis.shape[2]
    f32 = jnp.float32

    hots = [one_hot(leaf_order[i], leaf_size) for i in range(leaf_count)]
    ordered = jnp.stack(
        [
            jnp.dot(probes[i], hots[i], preferred_element_type=f32).astype(jnp.bfloat16)
            for i in range(leaf_count)
        ]
    )

    leaf_coef = lax.dot_general(
        ordered, leaf_basis, (((2,), (1,)), ((0,), (0,))), preferred_element_type=f32
    ).astype(jnp.bfloat16)
    stacked = leaf_coef.transpose(1, 0, 2).reshape(probe_count, leaf_count * skeleton)
    transfer_flat = node_transfer[0].reshape(leaf_count * skeleton, skeleton)
    node_coef = jnp.dot(stacked, transfer_flat, preferred_element_type=f32).astype(jnp.bfloat16)
    group_term = jnp.dot(node_coef, group_transfer[0], preferred_element_type=f32)
    node_index = lax.axis_index(DEV)
    node_total = lax.axis_size(DEV)

    probes_halo = with_halo(ordered, GROUP_DEV, NEAR_REACH)
    points_halo = with_halo(points, GROUP_DEV, NEAR_REACH)
    wide = leaf_count + 2 * NEAR_REACH
    own = range(NEAR_REACH, NEAR_REACH + leaf_count)
    pattern = near_pattern.astype(f32)
    jobs = [(b, b) for b in own]
    cross, inner = [], []
    for gap in range(1, NEAR_REACH + 1):
        for a in range(wide - gap):
            b = a + gap
            if a in own and b in own:
                inner.append((a, b))
            elif a in own:
                cross.append((a, b))
    jobs += cross + inner
    near = [jnp.zeros((probe_count, leaf_size), f32) for _ in range(leaf_count)]
    outgoing = {}

    def run_job(job, at, values):
        a, b = job
        tile = matern(at[a], at[b], signal_variance)
        if a == b:
            t = b - NEAR_REACH
            near[t] = near[t] + jnp.dot(values[b], tile, preferred_element_type=f32) * pattern[
                t, NEAR_REACH
            ]
            return
        gap = b - a
        if a in own and b in own:
            tile = lax.optimization_barrier(tile)
        if b in own:
            t = b - NEAR_REACH
            near[t] = near[t] + jnp.dot(
                values[a], tile, preferred_element_type=f32
            ) * pattern[t, NEAR_REACH - gap]
        if a in own:
            t = a - NEAR_REACH
            near[t] = near[t] + lax.dot_general(
                values[b], tile, (((1,), (1,)), ((), ())), preferred_element_type=f32
            ) * pattern[t, NEAR_REACH + gap]
        if b not in own:
            outgoing[job] = jnp.dot(values[a], tile, preferred_element_type=f32)

    rounds = ["dev_1", "dev_2", "dev_0"]
    steps = len(rounds) + 1
    running = group_term
    extra = node_coef.astype(f32)[None]
    block = lax.axis_size("dev_2")
    row = block * lax.axis_size("dev_1")
    group_index = lax.axis_index("group")
    group_total = lax.axis_size("group")
    for step in range(steps):
        chunk = jobs[step * len(jobs) // steps : (step + 1) * len(jobs) // steps]
        if any(job in cross for job in chunk):
            running, extra, points_of, probes_of, points_halo, probes_halo = (
                lax.optimization_barrier(
                    (running, extra, points, ordered, points_halo, probes_halo)
                )
            )
            at = spread_out(points_of, points_halo, NEAR_REACH)
            values = spread_out(probes_of, probes_halo, NEAR_REACH)
        else:
            running, extra, at, values = lax.optimization_barrier((running, extra, points, ordered))
            at = {b: at[b - NEAR_REACH] for b in own}
            values = {b: values[b - NEAR_REACH] for b in own}
        if step < len(rounds):
            received = from_everyone(jnp.concatenate([running[None], extra]), rounds[step])
        else:
            own_coef = running.astype(jnp.bfloat16)
            group_coef = from_everyone(own_coef, "group")
        for job in chunk:
            run_job(job, at, values)
        if step < len(rounds):
            running = jnp.sum(received[:, 0], axis=0)
            if step == 0:
                extra = received[:, 1]
            elif step == 1:
                row_coef = received[:, 1:].transpose(1, 0, 2, 3).reshape(row, probe_count, skeleton)
                extra = jnp.concatenate([row_coef[:COUPLE_REACH], row_coef[row - COUPLE_REACH :]])
            else:
                ends_coef = received[:, 1:]
    incoming = lax.ppermute(
        jnp.stack([outgoing[job] for job in cross]),
        GROUP_DEV,
        [(i, i + 1) for i in range(lax.axis_size(GROUP_DEV) - 1)],
    )
    for k, (a, b) in enumerate(cross):
        t = b - NEAR_REACH - leaf_count
        near[t] = near[t] + incoming[k] * pattern[t, NEAR_REACH - (b - a)]
    near = jnp.stack(near)

    own_skeleton = lax.dynamic_index_in_dim(group_skeleton, group_index, 0, keepdims=False)
    group_tiles = matern(
        group_skeleton.transpose(1, 0, 2).reshape(3, group_total * skeleton),
        own_skeleton,
        signal_variance,
    )
    others = lax.broadcasted_iota(jnp.int32, (group_total, 1, 1), 0) != group_index
    group_stack = jnp.where(others, group_coef, jnp.zeros_like(group_coef))
    group_stack = group_stack.transpose(1, 0, 2).reshape(probe_count, group_total * skeleton)
    far_group = jnp.dot(group_stack, group_tiles, preferred_element_type=f32)
    group_local = far_group.astype(jnp.bfloat16)

    own_node = lax.dynamic_index_in_dim(node_skeleton, node_index, 0, keepdims=False)
    ends = ends_coef.shape[1]
    table = jnp.concatenate([row_coef, ends_coef.reshape(-1, probe_count, skeleton)])
    line = node_index // row
    lines = lax.axis_size("dev_0")
    partner_points, picks, usable = [], [], []
    for offset in range(-COUPLE_REACH, COUPLE_REACH + 1):
        if abs(offset) < 2:
            continue
        partner = node_index + offset
        usable.append(
            (partner >= 0) & (partner < node_total) & (node_coupling[0, offset + COUPLE_REACH] > 0)
        )
        clamped = jnp.clip(partner, 0, node_total - 1)
        partner_points.append(lax.dynamic_index_in_dim(node_skeleton, clamped, 0, keepdims=False))
        along = node_index % row + offset
        same = jnp.clip(along, 0, row - 1)
        below = row + jnp.clip(line - 1, 0, lines - 1) * ends + COUPLE_REACH
        below = below + jnp.clip(along + COUPLE_REACH, 0, COUPLE_REACH - 1)
        above = row + jnp.clip(line + 1, 0, lines - 1) * ends
        above = above + jnp.clip(along - row, 0, COUPLE_REACH - 1)
        picks.append(jnp.where(along < 0, below, jnp.where(along >= row, above, same)))
    picked = jnp.take(table, jnp.stack(picks), axis=0)
    picked = jnp.where(jnp.stack(usable)[:, None, None], picked, jnp.zeros_like(picked))
    picked = picked.astype(jnp.bfloat16).transpose(1, 0, 2).reshape(probe_count, -1)
    couple_tiles = matern(jnp.concatenate(partner_points, axis=1), own_node, signal_variance)
    far_node = jnp.dot(picked, couple_tiles, preferred_element_type=f32)

    pushed = lax.dot_general(
        group_local, group_transfer[0], (((1,), (1,)), ((), ())), preferred_element_type=f32
    )
    node_local = (pushed + far_node).astype(jnp.bfloat16)
    spread = lax.dot_general(
        node_local, transfer_flat, (((1,), (1,)), ((), ())), preferred_element_type=f32
    )
    leaf_local = (
        spread.reshape(probe_count, leaf_count, skeleton).transpose(1, 0, 2).astype(jnp.bfloat16)
    )
    far_leaf = lax.dot_general(
        leaf_local, leaf_basis, (((2,), (2,)), ((0,), (0,))), preferred_element_type=f32
    )
    result = (far_leaf + near + noise_variance * ordered.astype(f32)).astype(jnp.bfloat16)
    restored = [
        lax.dot_general(
            result[i], hots[i], (((1,), (1,)), ((), ())), preferred_element_type=f32
        ).astype(jnp.bfloat16)
        for i in range(leaf_count)
    ]
    return jnp.stack(restored)


def solution(mesh):
    finer = Mesh(mesh.devices.reshape(mesh.shape["group"], 4, 4, 4), GROUP_DEV)
    return jax.shard_map(
        on_device,
        mesh=finer,
        in_specs=(
            P(GROUP_DEV, None, None),
            P(GROUP_DEV, None, None),
            P(GROUP_DEV, None),
            P(GROUP_DEV, None, None),
            P(GROUP_DEV, None, None, None),
            P(GROUP_DEV, None, None),
            P("group", None, None),
            P(),
            P(GROUP_DEV, None),
            P(GROUP_DEV, None),
            P(),
            P(),
        ),
        out_specs=P(GROUP_DEV, None, None),
        check_vma=False,
    )
```

```python
import jax
import jax.numpy as jnp
from jax import lax
from jax.sharding import Mesh
from jax.sharding import PartitionSpec as P

NEAR_REACH = 2
COUPLE_REACH = 4
GROUP_DEV = ("group", "dev_0", "dev_1", "dev_2")
DEV = ("dev_0", "dev_1", "dev_2")


ROOT_THREE = 1.7320508075688772
LENGTH_SCALE = 0.5


def with_halo(value, axis, width):
    peers, length = (lax.axis_size(axis), value.shape[0])
    up = [(i, i + 1) for i in range(peers - 1)]
    leading = value[:width]
    return lax.ppermute(leading, axis, [(b, a) for a, b in up])


def spread_out(value, high, width):
    pieces = [value[i] for i in range(value.shape[0])] + [high[i] for i in range(high.shape[0])]
    return dict(enumerate(pieces, start=width))


def from_behind(block, axis, distance):
    devices = range(lax.axis_size(axis))
    route = [(i - distance, i) for i in devices if i - distance in devices]
    return lax.ppermute(block, axis, route)


def tree_sum(value, axis):
    peers = lax.axis_size(axis)
    step = 1
    while step < peers:
        value = value + lax.ppermute(value, axis, [(i, i ^ step) for i in range(peers)])
        step *= 2
    return value


def from_everyone(value, axis):
    peers = lax.axis_size(axis)
    return lax.all_to_all(
        jnp.broadcast_to(value[None], (peers, *value.shape)), axis, 0, 0, tiled=True
    )


def cyclic_from_behind(block, axis, distance):
    peers = lax.axis_size(axis)
    return lax.ppermute(block, axis, [(i, (i + distance) % peers) for i in range(peers)])


def matern(source, target, amplitude):
    square = (source[0][:, None] - target[0][None, :]) ** 2
    square = square + (source[1][:, None] - target[1][None, :]) ** 2
    square = square + (source[2][:, None] - target[2][None, :]) ** 2
    scaled = jnp.sqrt(square) * (ROOT_THREE / LENGTH_SCALE)
    return (amplitude * (1.0 + scaled) * jnp.exp(-scaled)).astype(jnp.bfloat16)


def one_hot(ordering, size):
    rows = lax.broadcasted_iota(jnp.int32, (size, size), 0)
    return (rows == ordering[None, :]).astype(jnp.bfloat16)


def on_device(
    probes,
    points,
    leaf_order,
    leaf_basis,
    node_transfer,
    group_transfer,
    node_skeleton,
    group_skeleton,
    near_pattern,
    node_coupling,
    signal_variance,
    noise_variance,
):
    leaf_count, probe_count, leaf_size = probes.shape
    skeleton = leaf_basis.shape[2]
    f32 = jnp.float32

    hots = jax.vmap(lambda ordering: one_hot(ordering, leaf_size))(leaf_order)
    ordered = lax.dot_general(
        probes, hots, (((2,), (1,)), ((0,), (0,))), preferred_element_type=f32
    ).astype(jnp.bfloat16)

    leaf_coef = lax.dot_general(
        ordered, leaf_basis, (((2,), (1,)), ((0,), (0,))), preferred_element_type=f32
    ).astype(jnp.bfloat16)
    stacked = leaf_coef.transpose(1, 0, 2).reshape(probe_count, leaf_count * skeleton)
    transfer_flat = node_transfer[0].reshape(leaf_count * skeleton, skeleton)
    node_coef = jnp.dot(stacked, transfer_flat, preferred_element_type=f32).astype(jnp.bfloat16)
    group_term = jnp.dot(node_coef, group_transfer[0], preferred_element_type=f32)
    node_index = lax.axis_index(DEV)
    node_total = lax.axis_size(DEV)

    probes_halo = with_halo(ordered, GROUP_DEV, NEAR_REACH)
    points_halo = with_halo(points, GROUP_DEV, NEAR_REACH)
    wide = leaf_count + 2 * NEAR_REACH
    own = range(NEAR_REACH, NEAR_REACH + leaf_count)
    pattern = near_pattern.astype(f32)
    jobs = [(b, b) for b in own]
    cross, inner = [], []
    for gap in range(1, NEAR_REACH + 1):
        for a in range(wide - gap):
            b = a + gap
            if a in own and b in own:
                inner.append((a, b))
            elif a in own:
                cross.append((a, b))
    jobs += cross + inner
    near = [jnp.zeros((probe_count, leaf_size), f32) for _ in range(leaf_count)]
    outgoing = {}

    def run_job(job, at, values):
        a, b = job
        tile = matern(at[a], at[b], signal_variance)
        if a == b:
            t = b - NEAR_REACH
            near[t] = near[t] + jnp.dot(values[b], tile, preferred_element_type=f32) * pattern[
                t, NEAR_REACH
            ]
            return
        gap = b - a
        if a in own and b in own:
            tile = lax.optimization_barrier(tile)
        if b in own:
            t = b - NEAR_REACH
            near[t] = near[t] + jnp.dot(
                values[a], tile, preferred_element_type=f32
            ) * pattern[t, NEAR_REACH - gap]
        if a in own:
            t = a - NEAR_REACH
            near[t] = near[t] + lax.dot_general(
                values[b], tile, (((1,), (1,)), ((), ())), preferred_element_type=f32
            ) * pattern[t, NEAR_REACH + gap]
        if b not in own:
            outgoing[job] = jnp.dot(values[a], tile, preferred_element_type=f32)

    rounds = ["dev_1", "dev_2", "dev_0"]
    steps = len(rounds) + 1
    running = group_term
    extra = node_coef.astype(f32)[None]
    block = lax.axis_size("dev_2")
    row = block * lax.axis_size("dev_1")
    group_index = lax.axis_index("group")
    group_total = lax.axis_size("group")
    for step in range(steps):
        chunk = jobs[step * len(jobs) // steps : (step + 1) * len(jobs) // steps]
        if any(job in cross for job in chunk):
            running, extra, points_of, probes_of, points_halo, probes_halo = (
                lax.optimization_barrier(
                    (running, extra, points, ordered, points_halo, probes_halo)
                )
            )
            at = spread_out(points_of, points_halo, NEAR_REACH)
            values = spread_out(probes_of, probes_halo, NEAR_REACH)
        else:
            running, extra, at, values = lax.optimization_barrier((running, extra, points, ordered))
            at = {b: at[b - NEAR_REACH] for b in own}
            values = {b: values[b - NEAR_REACH] for b in own}
        if step < len(rounds):
            received = from_everyone(jnp.concatenate([running[None], extra]), rounds[step])
        else:
            own_coef = running.astype(jnp.bfloat16)
            group_coef = from_everyone(own_coef, "group")
        for job in chunk:
            run_job(job, at, values)
        if step < len(rounds):
            running = jnp.sum(received[:, 0], axis=0)
            if step == 0:
                extra = received[:, 1]
            elif step == 1:
                row_coef = received[:, 1:].transpose(1, 0, 2, 3).reshape(row, probe_count, skeleton)
                extra = jnp.concatenate([row_coef[:COUPLE_REACH], row_coef[row - COUPLE_REACH :]])
            else:
                ends_coef = received[:, 1:]
    incoming = lax.ppermute(
        jnp.stack([outgoing[job] for job in cross]),
        GROUP_DEV,
        [(i, i + 1) for i in range(lax.axis_size(GROUP_DEV) - 1)],
    )
    for k, (a, b) in enumerate(cross):
        t = b - NEAR_REACH - leaf_count
        near[t] = near[t] + incoming[k] * pattern[t, NEAR_REACH - (b - a)]
    near = jnp.stack(near)

    own_skeleton = lax.dynamic_index_in_dim(group_skeleton, group_index, 0, keepdims=False)
    group_tiles = matern(
        group_skeleton.transpose(1, 0, 2).reshape(3, group_total * skeleton),
        own_skeleton,
        signal_variance,
    )
    others = lax.broadcasted_iota(jnp.int32, (group_total, 1, 1), 0) != group_index
    group_stack = jnp.where(others, group_coef, jnp.zeros_like(group_coef))
    group_stack = group_stack.transpose(1, 0, 2).reshape(probe_count, group_total * skeleton)
    far_group = jnp.dot(group_stack, group_tiles, preferred_element_type=f32)
    group_local = far_group.astype(jnp.bfloat16)

    own_node = lax.dynamic_index_in_dim(node_skeleton, node_index, 0, keepdims=False)
    ends = ends_coef.shape[1]
    table = jnp.concatenate([row_coef, ends_coef.reshape(-1, probe_count, skeleton)])
    line = node_index // row
    lines = lax.axis_size("dev_0")
    partner_points, picks, usable = [], [], []
    for offset in range(-COUPLE_REACH, COUPLE_REACH + 1):
        if abs(offset) < 2:
            continue
        partner = node_index + offset
        usable.append(
            (partner >= 0) & (partner < node_total) & (node_coupling[0, offset + COUPLE_REACH] > 0)
        )
        clamped = jnp.clip(partner, 0, node_total - 1)
        partner_points.append(lax.dynamic_index_in_dim(node_skeleton, clamped, 0, keepdims=False))
        along = node_index % row + offset
        same = jnp.clip(along, 0, row - 1)
        below = row + jnp.clip(line - 1, 0, lines - 1) * ends + COUPLE_REACH
        below = below + jnp.clip(along + COUPLE_REACH, 0, COUPLE_REACH - 1)
        above = row + jnp.clip(line + 1, 0, lines - 1) * ends
        above = above + jnp.clip(along - row, 0, COUPLE_REACH - 1)
        picks.append(jnp.where(along < 0, below, jnp.where(along >= row, above, same)))
    picked = jnp.take(table, jnp.stack(picks), axis=0)
    picked = jnp.where(jnp.stack(usable)[:, None, None], picked, jnp.zeros_like(picked))
    picked = picked.astype(jnp.bfloat16).transpose(1, 0, 2).reshape(probe_count, -1)
    couple_tiles = matern(jnp.concatenate(partner_points, axis=1), own_node, signal_variance)
    far_node = jnp.dot(picked, couple_tiles, preferred_element_type=f32)

    pushed = lax.dot_general(
        group_local, group_transfer[0], (((1,), (1,)), ((), ())), preferred_element_type=f32
    )
    node_local = (pushed + far_node).astype(jnp.bfloat16)
    spread = lax.dot_general(
        node_local, transfer_flat, (((1,), (1,)), ((), ())), preferred_element_type=f32
    )
    leaf_local = (
        spread.reshape(probe_count, leaf_count, skeleton).transpose(1, 0, 2).astype(jnp.bfloat16)
    )
    far_leaf = lax.dot_general(
        leaf_local, leaf_basis, (((2,), (2,)), ((0,), (0,))), preferred_element_type=f32
    )
    result = (far_leaf + near + noise_variance * ordered.astype(f32)).astype(jnp.bfloat16)
    restored = lax.dot_general(
        result, hots, (((2,), (2,)), ((0,), (0,))), preferred_element_type=f32
    )
    return restored.astype(jnp.bfloat16)


def solution(mesh):
    finer = Mesh(mesh.devices.reshape(mesh.shape["group"], 4, 4, 4), GROUP_DEV)
    return jax.shard_map(
        on_device,
        mesh=finer,
        in_specs=(
            P(GROUP_DEV, None, None),
            P(GROUP_DEV, None, None),
            P(GROUP_DEV, None),
            P(GROUP_DEV, None, None),
            P(GROUP_DEV, None, None, None),
            P(GROUP_DEV, None, None),
            P("group", None, None),
            P(),
            P(GROUP_DEV, None),
            P(GROUP_DEV, None),
            P(),
            P(),
        ),
        out_specs=P(GROUP_DEV, None, None),
        check_vma=False,
    )
```

```python
import jax
import jax.numpy as jnp
from jax import lax
from jax.sharding import Mesh
from jax.sharding import PartitionSpec as P

NEAR_REACH = 2
COUPLE_REACH = 4
GROUP_DEV = ("group", "dev_0", "dev_1", "dev_2")
DEV = ("dev_0", "dev_1", "dev_2")


ROOT_THREE = 1.7320508075688772
LENGTH_SCALE = 0.5


def with_halo(value, axis, width):
    peers, length = (lax.axis_size(axis), value.shape[0])
    up = [(i, i + 1) for i in range(peers - 1)]
    leading = value[:width]
    return lax.ppermute(leading, axis, [(b, a) for a, b in up])


def spread_out(value, high, width):
    pieces = [value[i] for i in range(value.shape[0])] + [high[i] for i in range(high.shape[0])]
    return dict(enumerate(pieces, start=width))


def from_behind(block, axis, distance):
    devices = range(lax.axis_size(axis))
    route = [(i - distance, i) for i in devices if i - distance in devices]
    return lax.ppermute(block, axis, route)


def tree_sum(value, axis):
    peers = lax.axis_size(axis)
    step = 1
    while step < peers:
        value = value + lax.ppermute(value, axis, [(i, i ^ step) for i in range(peers)])
        step *= 2
    return value


def from_everyone(value, axis):
    peers = lax.axis_size(axis)
    return lax.all_to_all(
        jnp.broadcast_to(value[None], (peers, *value.shape)), axis, 0, 0, tiled=True
    )


def cyclic_from_behind(block, axis, distance):
    peers = lax.axis_size(axis)
    return lax.ppermute(block, axis, [(i, (i + distance) % peers) for i in range(peers)])


def matern(source, target, amplitude):
    square = (source[0][:, None] - target[0][None, :]) ** 2
    square = square + (source[1][:, None] - target[1][None, :]) ** 2
    square = square + (source[2][:, None] - target[2][None, :]) ** 2
    scaled = jnp.sqrt(square) * (ROOT_THREE / LENGTH_SCALE)
    return (amplitude * (1.0 + scaled) * jnp.exp(-scaled)).astype(jnp.bfloat16)


def one_hot(ordering, size):
    rows = lax.broadcasted_iota(jnp.int32, (size, size), 0)
    return (rows == ordering[None, :]).astype(jnp.bfloat16)


def on_device(
    probes,
    points,
    leaf_order,
    leaf_basis,
    node_transfer,
    group_transfer,
    node_skeleton,
    group_skeleton,
    near_pattern,
    node_coupling,
    signal_variance,
    noise_variance,
):
    leaf_count, probe_count, leaf_size = probes.shape
    skeleton = leaf_basis.shape[2]
    f32 = jnp.float32

    hots = jax.vmap(lambda ordering: one_hot(ordering, leaf_size))(leaf_order)
    ordered = lax.dot_general(
        probes, hots, (((2,), (1,)), ((0,), (0,))), preferred_element_type=f32
    ).astype(jnp.bfloat16)

    leaf_coef = lax.dot_general(
        ordered, leaf_basis, (((2,), (1,)), ((0,), (0,))), preferred_element_type=f32
    ).astype(jnp.bfloat16)
    stacked = leaf_coef.transpose(1, 0, 2).reshape(probe_count, leaf_count * skeleton)
    transfer_flat = node_transfer[0].reshape(leaf_count * skeleton, skeleton)
    node_coef = jnp.dot(stacked, transfer_flat, preferred_element_type=f32).astype(jnp.bfloat16)
    group_term = jnp.dot(node_coef, group_transfer[0], preferred_element_type=f32)
    node_index = lax.axis_index(DEV)
    node_total = lax.axis_size(DEV)

    probes_halo = with_halo(ordered, GROUP_DEV, NEAR_REACH)
    points_halo = with_halo(points, GROUP_DEV, NEAR_REACH)
    wide = leaf_count + 2 * NEAR_REACH
    own = range(NEAR_REACH, NEAR_REACH + leaf_count)
    pattern = near_pattern.astype(f32)
    jobs = [(b, b) for b in own]
    cross, inner = [], []
    for gap in range(1, NEAR_REACH + 1):
        for a in range(wide - gap):
            b = a + gap
            if a in own and b in own:
                inner.append((a, b))
            elif a in own:
                cross.append((a, b))
    jobs += cross + inner
    near = [jnp.zeros((probe_count, leaf_size), f32) for _ in range(leaf_count)]
    outgoing = {}

    def run_job(job, at, values):
        a, b = job
        tile = lax.optimization_barrier(matern(at[a], at[b], signal_variance))
        if a == b:
            t = b - NEAR_REACH
            near[t] = near[t] + jnp.dot(values[b], tile, preferred_element_type=f32) * pattern[
                t, NEAR_REACH
            ]
            return
        gap = b - a
        if b in own:
            t = b - NEAR_REACH
            near[t] = near[t] + jnp.dot(
                values[a], tile, preferred_element_type=f32
            ) * pattern[t, NEAR_REACH - gap]
        if a in own:
            t = a - NEAR_REACH
            near[t] = near[t] + lax.dot_general(
                values[b], tile, (((1,), (1,)), ((), ())), preferred_element_type=f32
            ) * pattern[t, NEAR_REACH + gap]
        if b not in own:
            outgoing[job] = jnp.dot(values[a], tile, preferred_element_type=f32)

    rounds = ["dev_1", "dev_2", "dev_0"]
    steps = len(rounds) + 1
    running = group_term
    extra = node_coef.astype(f32)[None]
    block = lax.axis_size("dev_2")
    row = block * lax.axis_size("dev_1")
    group_index = lax.axis_index("group")
    group_total = lax.axis_size("group")
    for step in range(steps):
        chunk = jobs[step * len(jobs) // steps : (step + 1) * len(jobs) // steps]
        if any(job in cross for job in chunk):
            running, extra, points_of, probes_of, points_halo, probes_halo = (
                lax.optimization_barrier(
                    (running, extra, points, ordered, points_halo, probes_halo)
                )
            )
            at = spread_out(points_of, points_halo, NEAR_REACH)
            values = spread_out(probes_of, probes_halo, NEAR_REACH)
        else:
            running, extra, at, values = lax.optimization_barrier((running, extra, points, ordered))
            at = {b: at[b - NEAR_REACH] for b in own}
            values = {b: values[b - NEAR_REACH] for b in own}
        if step < len(rounds):
            received = from_everyone(jnp.concatenate([running[None], extra]), rounds[step])
        else:
            own_coef = running.astype(jnp.bfloat16)
            group_coef = from_everyone(own_coef, "group")
        for job in chunk:
            run_job(job, at, values)
        if step < len(rounds):
            running = jnp.sum(received[:, 0], axis=0)
            if step == 0:
                extra = received[:, 1]
            elif step == 1:
                row_coef = received[:, 1:].transpose(1, 0, 2, 3).reshape(row, probe_count, skeleton)
                extra = jnp.concatenate([row_coef[:COUPLE_REACH], row_coef[row - COUPLE_REACH :]])
            else:
                ends_coef = received[:, 1:]
    incoming = lax.ppermute(
        jnp.stack([outgoing[job] for job in cross]),
        GROUP_DEV,
        [(i, i + 1) for i in range(lax.axis_size(GROUP_DEV) - 1)],
    )
    for k, (a, b) in enumerate(cross):
        t = b - NEAR_REACH - leaf_count
        near[t] = near[t] + incoming[k] * pattern[t, NEAR_REACH - (b - a)]
    near = jnp.stack(near)

    own_skeleton = lax.dynamic_index_in_dim(group_skeleton, group_index, 0, keepdims=False)
    group_tiles = matern(
        group_skeleton.transpose(1, 0, 2).reshape(3, group_total * skeleton),
        own_skeleton,
        signal_variance,
    )
    others = lax.broadcasted_iota(jnp.int32, (group_total, 1, 1), 0) != group_index
    group_stack = jnp.where(others, group_coef, jnp.zeros_like(group_coef))
    group_stack = group_stack.transpose(1, 0, 2).reshape(probe_count, group_total * skeleton)
    far_group = jnp.dot(group_stack, group_tiles, preferred_element_type=f32)
    group_local = far_group.astype(jnp.bfloat16)

    own_node = lax.dynamic_index_in_dim(node_skeleton, node_index, 0, keepdims=False)
    ends = ends_coef.shape[1]
    table = jnp.concatenate([row_coef, ends_coef.reshape(-1, probe_count, skeleton)])
    line = node_index // row
    lines = lax.axis_size("dev_0")
    partner_points, picks, usable = [], [], []
    for offset in range(-COUPLE_REACH, COUPLE_REACH + 1):
        if abs(offset) < 2:
            continue
        partner = node_index + offset
        usable.append(
            (partner >= 0) & (partner < node_total) & (node_coupling[0, offset + COUPLE_REACH] > 0)
        )
        clamped = jnp.clip(partner, 0, node_total - 1)
        partner_points.append(lax.dynamic_index_in_dim(node_skeleton, clamped, 0, keepdims=False))
        along = node_index % row + offset
        same = jnp.clip(along, 0, row - 1)
        below = row + jnp.clip(line - 1, 0, lines - 1) * ends + COUPLE_REACH
        below = below + jnp.clip(along + COUPLE_REACH, 0, COUPLE_REACH - 1)
        above = row + jnp.clip(line + 1, 0, lines - 1) * ends
        above = above + jnp.clip(along - row, 0, COUPLE_REACH - 1)
        picks.append(jnp.where(along < 0, below, jnp.where(along >= row, above, same)))
    picked = jnp.take(table, jnp.stack(picks), axis=0)
    picked = jnp.where(jnp.stack(usable)[:, None, None], picked, jnp.zeros_like(picked))
    picked = picked.astype(jnp.bfloat16).transpose(1, 0, 2).reshape(probe_count, -1)
    couple_tiles = matern(jnp.concatenate(partner_points, axis=1), own_node, signal_variance)
    far_node = jnp.dot(picked, couple_tiles, preferred_element_type=f32)

    pushed = lax.dot_general(
        group_local, group_transfer[0], (((1,), (1,)), ((), ())), preferred_element_type=f32
    )
    node_local = (pushed + far_node).astype(jnp.bfloat16)
    spread = lax.dot_general(
        node_local, transfer_flat, (((1,), (1,)), ((), ())), preferred_element_type=f32
    )
    leaf_local = (
        spread.reshape(probe_count, leaf_count, skeleton).transpose(1, 0, 2).astype(jnp.bfloat16)
    )
    far_leaf = lax.dot_general(
        leaf_local, leaf_basis, (((2,), (2,)), ((0,), (0,))), preferred_element_type=f32
    )
    result = (far_leaf + near + noise_variance * ordered.astype(f32)).astype(jnp.bfloat16)
    restored = lax.dot_general(
        result, hots, (((2,), (2,)), ((0,), (0,))), preferred_element_type=f32
    )
    return restored.astype(jnp.bfloat16)


def solution(mesh):
    finer = Mesh(mesh.devices.reshape(mesh.shape["group"], 4, 4, 4), GROUP_DEV)
    return jax.shard_map(
        on_device,
        mesh=finer,
        in_specs=(
            P(GROUP_DEV, None, None),
            P(GROUP_DEV, None, None),
            P(GROUP_DEV, None),
            P(GROUP_DEV, None, None),
            P(GROUP_DEV, None, None, None),
            P(GROUP_DEV, None, None),
            P("group", None, None),
            P(),
            P(GROUP_DEV, None),
            P(GROUP_DEV, None),
            P(),
            P(),
        ),
        out_specs=P(GROUP_DEV, None, None),
        check_vma=False,
    )
```

```python
import jax
import jax.numpy as jnp
from jax import lax
from jax.sharding import Mesh
from jax.sharding import PartitionSpec as P

NEAR_REACH = 2
COUPLE_REACH = 4
GROUP_DEV = ("group", "dev_0", "dev_1", "dev_2")
DEV = ("dev_0", "dev_1", "dev_2")


ROOT_THREE = 1.7320508075688772
LENGTH_SCALE = 0.5


def with_halo(value, axis, width):
    peers, length = (lax.axis_size(axis), value.shape[0])
    up = [(i, i + 1) for i in range(peers - 1)]
    leading = value[:width]
    return lax.ppermute(leading, axis, [(b, a) for a, b in up])


def spread_out(value, high, width):
    pieces = [value[i] for i in range(value.shape[0])] + [high[i] for i in range(high.shape[0])]
    return dict(enumerate(pieces, start=width))


def from_behind(block, axis, distance):
    devices = range(lax.axis_size(axis))
    route = [(i - distance, i) for i in devices if i - distance in devices]
    return lax.ppermute(block, axis, route)


def tree_sum(value, axis):
    peers = lax.axis_size(axis)
    step = 1
    while step < peers:
        value = value + lax.ppermute(value, axis, [(i, i ^ step) for i in range(peers)])
        step *= 2
    return value


def from_everyone(value, axis):
    peers = lax.axis_size(axis)
    return lax.all_to_all(
        jnp.broadcast_to(value[None], (peers, *value.shape)), axis, 0, 0, tiled=True
    )


def cyclic_from_behind(block, axis, distance):
    peers = lax.axis_size(axis)
    return lax.ppermute(block, axis, [(i, (i + distance) % peers) for i in range(peers)])


def matern(source, target, amplitude):
    square = (source[0][:, None] - target[0][None, :]) ** 2
    square = square + (source[1][:, None] - target[1][None, :]) ** 2
    square = square + (source[2][:, None] - target[2][None, :]) ** 2
    scaled = jnp.sqrt(square) * (ROOT_THREE / LENGTH_SCALE)
    return (amplitude * (1.0 + scaled) * jnp.exp(-scaled)).astype(jnp.bfloat16)


def one_hot(ordering, size):
    rows = lax.broadcasted_iota(jnp.int32, (size, size), 0)
    return (rows == ordering[None, :]).astype(jnp.bfloat16)


def on_device(
    probes,
    points,
    leaf_order,
    leaf_basis,
    node_transfer,
    group_transfer,
    node_skeleton,
    group_skeleton,
    near_pattern,
    node_coupling,
    signal_variance,
    noise_variance,
):
    leaf_count, probe_count, leaf_size = probes.shape
    skeleton = leaf_basis.shape[2]
    f32 = jnp.float32

    hots = jax.vmap(lambda ordering: one_hot(ordering, leaf_size))(leaf_order)
    ordered = lax.dot_general(
        probes, hots, (((2,), (1,)), ((0,), (0,))), preferred_element_type=f32
    ).astype(jnp.bfloat16)

    leaf_coef = lax.dot_general(
        ordered, leaf_basis, (((2,), (1,)), ((0,), (0,))), preferred_element_type=f32
    ).astype(jnp.bfloat16)
    stacked = leaf_coef.transpose(1, 0, 2).reshape(probe_count, leaf_count * skeleton)
    transfer_flat = node_transfer[0].reshape(leaf_count * skeleton, skeleton)
    node_coef = jnp.dot(stacked, transfer_flat, preferred_element_type=f32).astype(jnp.bfloat16)
    group_term = jnp.dot(node_coef, group_transfer[0], preferred_element_type=f32)
    node_index = lax.axis_index(DEV)
    node_total = lax.axis_size(DEV)

    probes_halo = with_halo(ordered, GROUP_DEV, NEAR_REACH)
    points_halo = with_halo(points, GROUP_DEV, NEAR_REACH)
    wide = leaf_count + 2 * NEAR_REACH
    own = range(NEAR_REACH, NEAR_REACH + leaf_count)
    pattern = near_pattern.astype(f32)
    jobs = [(b, b) for b in own]
    cross, inner = [], []
    for gap in range(1, NEAR_REACH + 1):
        for a in range(wide - gap):
            b = a + gap
            if a in own and b in own:
                inner.append((a, b))
            elif a in own:
                cross.append((a, b))
    jobs += cross + inner
    near = [jnp.zeros((probe_count, leaf_size), f32) for _ in range(leaf_count)]
    outgoing = {}

    def run_job(job, at, values):
        a, b = job
        tile = lax.optimization_barrier(matern(at[a], at[b], signal_variance))
        if a == b:
            t = b - NEAR_REACH
            near[t] = near[t] + lax.dot_general(
                values[b], tile, (((1,), (1,)), ((), ())), preferred_element_type=f32
            ) * pattern[t, NEAR_REACH]
            return
        gap = b - a
        if b in own:
            t = b - NEAR_REACH
            near[t] = near[t] + jnp.dot(
                values[a], tile, preferred_element_type=f32
            ) * pattern[t, NEAR_REACH - gap]
        if a in own:
            t = a - NEAR_REACH
            near[t] = near[t] + lax.dot_general(
                values[b], tile, (((1,), (1,)), ((), ())), preferred_element_type=f32
            ) * pattern[t, NEAR_REACH + gap]
        if b not in own:
            outgoing[job] = jnp.dot(values[a], tile, preferred_element_type=f32)

    rounds = ["dev_1", "dev_2", "dev_0"]
    steps = len(rounds) + 1
    running = group_term
    extra = node_coef.astype(f32)[None]
    block = lax.axis_size("dev_2")
    row = block * lax.axis_size("dev_1")
    group_index = lax.axis_index("group")
    group_total = lax.axis_size("group")
    for step in range(steps):
        chunk = jobs[step * len(jobs) // steps : (step + 1) * len(jobs) // steps]
        if any(job in cross for job in chunk):
            running, extra, points_of, probes_of, points_halo, probes_halo = (
                lax.optimization_barrier(
                    (running, extra, points, ordered, points_halo, probes_halo)
                )
            )
            at = spread_out(points_of, points_halo, NEAR_REACH)
            values = spread_out(probes_of, probes_halo, NEAR_REACH)
        else:
            running, extra, at, values = lax.optimization_barrier((running, extra, points, ordered))
            at = {b: at[b - NEAR_REACH] for b in own}
            values = {b: values[b - NEAR_REACH] for b in own}
        if step < len(rounds):
            received = from_everyone(jnp.concatenate([running[None], extra]), rounds[step])
        else:
            own_coef = running.astype(jnp.bfloat16)
            group_coef = from_everyone(own_coef, "group")
        for job in chunk:
            run_job(job, at, values)
        if step < len(rounds):
            running = jnp.sum(received[:, 0], axis=0)
            if step == 0:
                extra = received[:, 1]
            elif step == 1:
                row_coef = received[:, 1:].transpose(1, 0, 2, 3).reshape(row, probe_count, skeleton)
                extra = jnp.concatenate([row_coef[:COUPLE_REACH], row_coef[row - COUPLE_REACH :]])
            else:
                ends_coef = received[:, 1:]
    incoming = lax.ppermute(
        jnp.stack([outgoing[job] for job in cross]),
        GROUP_DEV,
        [(i, i + 1) for i in range(lax.axis_size(GROUP_DEV) - 1)],
    )
    for k, (a, b) in enumerate(cross):
        t = b - NEAR_REACH - leaf_count
        near[t] = near[t] + incoming[k] * pattern[t, NEAR_REACH - (b - a)]
    near = jnp.stack(near)

    own_skeleton = lax.dynamic_index_in_dim(group_skeleton, group_index, 0, keepdims=False)
    group_tiles = matern(
        group_skeleton.transpose(1, 0, 2).reshape(3, group_total * skeleton),
        own_skeleton,
        signal_variance,
    )
    others = lax.broadcasted_iota(jnp.int32, (group_total, 1, 1), 0) != group_index
    group_stack = jnp.where(others, group_coef, jnp.zeros_like(group_coef))
    group_stack = group_stack.transpose(1, 0, 2).reshape(probe_count, group_total * skeleton)
    far_group = jnp.dot(group_stack, group_tiles, preferred_element_type=f32)
    group_local = far_group.astype(jnp.bfloat16)

    own_node = lax.dynamic_index_in_dim(node_skeleton, node_index, 0, keepdims=False)
    ends = ends_coef.shape[1]
    table = jnp.concatenate([row_coef, ends_coef.reshape(-1, probe_count, skeleton)])
    line = node_index // row
    lines = lax.axis_size("dev_0")
    partner_points, picks, usable = [], [], []
    for offset in range(-COUPLE_REACH, COUPLE_REACH + 1):
        if abs(offset) < 2:
            continue
        partner = node_index + offset
        usable.append(
            (partner >= 0) & (partner < node_total) & (node_coupling[0, offset + COUPLE_REACH] > 0)
        )
        clamped = jnp.clip(partner, 0, node_total - 1)
        partner_points.append(lax.dynamic_index_in_dim(node_skeleton, clamped, 0, keepdims=False))
        along = node_index % row + offset
        same = jnp.clip(along, 0, row - 1)
        below = row + jnp.clip(line - 1, 0, lines - 1) * ends + COUPLE_REACH
        below = below + jnp.clip(along + COUPLE_REACH, 0, COUPLE_REACH - 1)
        above = row + jnp.clip(line + 1, 0, lines - 1) * ends
        above = above + jnp.clip(along - row, 0, COUPLE_REACH - 1)
        picks.append(jnp.where(along < 0, below, jnp.where(along >= row, above, same)))
    picked = jnp.take(table, jnp.stack(picks), axis=0)
    picked = jnp.where(jnp.stack(usable)[:, None, None], picked, jnp.zeros_like(picked))
    picked = picked.astype(jnp.bfloat16).transpose(1, 0, 2).reshape(probe_count, -1)
    couple_tiles = matern(jnp.concatenate(partner_points, axis=1), own_node, signal_variance)
    far_node = jnp.dot(picked, couple_tiles, preferred_element_type=f32)

    pushed = lax.dot_general(
        group_local, group_transfer[0], (((1,), (1,)), ((), ())), preferred_element_type=f32
    )
    node_local = (pushed + far_node).astype(jnp.bfloat16)
    spread = lax.dot_general(
        node_local, transfer_flat, (((1,), (1,)), ((), ())), preferred_element_type=f32
    )
    leaf_local = (
        spread.reshape(probe_count, leaf_count, skeleton).transpose(1, 0, 2).astype(jnp.bfloat16)
    )
    far_leaf = lax.dot_general(
        leaf_local, leaf_basis, (((2,), (2,)), ((0,), (0,))), preferred_element_type=f32
    )
    result = (far_leaf + near + noise_variance * ordered.astype(f32)).astype(jnp.bfloat16)
    restored = lax.dot_general(
        result, hots, (((2,), (2,)), ((0,), (0,))), preferred_element_type=f32
    )
    return restored.astype(jnp.bfloat16)


def solution(mesh):
    finer = Mesh(mesh.devices.reshape(mesh.shape["group"], 4, 4, 4), GROUP_DEV)
    return jax.shard_map(
        on_device,
        mesh=finer,
        in_specs=(
            P(GROUP_DEV, None, None),
            P(GROUP_DEV, None, None),
            P(GROUP_DEV, None),
            P(GROUP_DEV, None, None),
            P(GROUP_DEV, None, None, None),
            P(GROUP_DEV, None, None),
            P("group", None, None),
            P(),
            P(GROUP_DEV, None),
            P(GROUP_DEV, None),
            P(),
            P(),
        ),
        out_specs=P(GROUP_DEV, None, None),
        check_vma=False,
    )
```

```python
import jax
import jax.numpy as jnp
from jax import lax
from jax.sharding import Mesh
from jax.sharding import PartitionSpec as P

NEAR_REACH = 2
COUPLE_REACH = 4
GROUP_DEV = ("group", "dev_0", "dev_1", "dev_2")
DEV = ("dev_0", "dev_1", "dev_2")


ROOT_THREE = 1.7320508075688772
LENGTH_SCALE = 0.5


def with_halo(value, axis, width):
    peers, length = (lax.axis_size(axis), value.shape[0])
    up = [(i, i + 1) for i in range(peers - 1)]
    leading = value[:width]
    return lax.ppermute(leading, axis, [(b, a) for a, b in up])


def spread_out(value, high, width):
    pieces = [value[i] for i in range(value.shape[0])] + [high[i] for i in range(high.shape[0])]
    return dict(enumerate(pieces, start=width))


def from_behind(block, axis, distance):
    devices = range(lax.axis_size(axis))
    route = [(i - distance, i) for i in devices if i - distance in devices]
    return lax.ppermute(block, axis, route)


def tree_sum(value, axis):
    peers = lax.axis_size(axis)
    step = 1
    while step < peers:
        value = value + lax.ppermute(value, axis, [(i, i ^ step) for i in range(peers)])
        step *= 2
    return value


def from_everyone(value, axis):
    peers = lax.axis_size(axis)
    return lax.all_to_all(
        jnp.broadcast_to(value[None], (peers, *value.shape)), axis, 0, 0, tiled=True
    )


def cyclic_from_behind(block, axis, distance):
    peers = lax.axis_size(axis)
    return lax.ppermute(block, axis, [(i, (i + distance) % peers) for i in range(peers)])


def matern(source, target, amplitude):
    square = (source[0][:, None] - target[0][None, :]) ** 2
    square = square + (source[1][:, None] - target[1][None, :]) ** 2
    square = square + (source[2][:, None] - target[2][None, :]) ** 2
    scaled = jnp.sqrt(square) * (ROOT_THREE / LENGTH_SCALE)
    return (amplitude * (1.0 + scaled) * jnp.exp(-scaled)).astype(jnp.bfloat16)


def one_hot(ordering, size):
    rows = lax.broadcasted_iota(jnp.int32, (size, size), 0)
    return (rows == ordering[None, :]).astype(jnp.bfloat16)


def on_device(
    probes,
    points,
    leaf_order,
    leaf_basis,
    node_transfer,
    group_transfer,
    node_skeleton,
    group_skeleton,
    near_pattern,
    node_coupling,
    signal_variance,
    noise_variance,
):
    leaf_count, probe_count, leaf_size = probes.shape
    skeleton = leaf_basis.shape[2]
    f32 = jnp.float32

    hots = jax.vmap(lambda ordering: one_hot(ordering, leaf_size))(leaf_order)
    ordered = lax.dot_general(
        probes, hots, (((2,), (1,)), ((0,), (0,))), preferred_element_type=f32
    ).astype(jnp.bfloat16)

    leaf_coef = lax.dot_general(
        ordered, leaf_basis, (((2,), (1,)), ((0,), (0,))), preferred_element_type=f32
    ).astype(jnp.bfloat16)
    stacked = leaf_coef.transpose(1, 0, 2).reshape(probe_count, leaf_count * skeleton)
    transfer_flat = node_transfer[0].reshape(leaf_count * skeleton, skeleton)
    node_coef = jnp.dot(stacked, transfer_flat, preferred_element_type=f32).astype(jnp.bfloat16)
    group_term = jnp.dot(node_coef, group_transfer[0], preferred_element_type=f32)
    node_index = lax.axis_index(DEV)
    node_total = lax.axis_size(DEV)

    probes_halo = with_halo(ordered, GROUP_DEV, NEAR_REACH)
    points_halo = with_halo(points, GROUP_DEV, NEAR_REACH)
    wide = leaf_count + 2 * NEAR_REACH
    own = range(NEAR_REACH, NEAR_REACH + leaf_count)
    pattern = near_pattern.astype(f32)
    jobs = [(b, b) for b in own]
    cross, inner = [], []
    for gap in range(1, NEAR_REACH + 1):
        for a in range(wide - gap):
            b = a + gap
            if a in own and b in own:
                inner.append((a, b))
            elif a in own:
                cross.append((a, b))
    jobs += cross + inner
    near = [jnp.zeros((probe_count, leaf_size), f32) for _ in range(leaf_count)]
    outgoing = {}

    def run_job(job, tile, values):
        a, b = job
        if a == b:
            t = b - NEAR_REACH
            near[t] = near[t] + jnp.dot(values[b], tile, preferred_element_type=f32) * pattern[
                t, NEAR_REACH
            ]
            return
        gap = b - a
        if b in own:
            t = b - NEAR_REACH
            near[t] = near[t] + jnp.dot(
                values[a], tile, preferred_element_type=f32
            ) * pattern[t, NEAR_REACH - gap]
        if a in own:
            t = a - NEAR_REACH
            near[t] = near[t] + lax.dot_general(
                values[b], tile, (((1,), (1,)), ((), ())), preferred_element_type=f32
            ) * pattern[t, NEAR_REACH + gap]
        if b not in own:
            outgoing[job] = jnp.dot(values[a], tile, preferred_element_type=f32)

    rounds = ["dev_1", "dev_2", "dev_0"]
    steps = len(rounds) + 1
    running = group_term
    extra = node_coef.astype(f32)[None]
    block = lax.axis_size("dev_2")
    row = block * lax.axis_size("dev_1")
    group_index = lax.axis_index("group")
    group_total = lax.axis_size("group")
    for step in range(steps):
        chunk = jobs[step * len(jobs) // steps : (step + 1) * len(jobs) // steps]
        if any(job in cross for job in chunk):
            running, extra, points_of, probes_of, points_halo, probes_halo = (
                lax.optimization_barrier(
                    (running, extra, points, ordered, points_halo, probes_halo)
                )
            )
            at = spread_out(points_of, points_halo, NEAR_REACH)
            values = spread_out(probes_of, probes_halo, NEAR_REACH)
        else:
            running, extra, at, values = lax.optimization_barrier((running, extra, points, ordered))
            at = {b: at[b - NEAR_REACH] for b in own}
            values = {b: values[b - NEAR_REACH] for b in own}
        if step < len(rounds):
            received = from_everyone(jnp.concatenate([running[None], extra]), rounds[step])
        else:
            own_coef = running.astype(jnp.bfloat16)
            group_coef = from_everyone(own_coef, "group")
        tiles = lax.optimization_barrier(
            tuple(matern(at[a], at[b], signal_variance) for a, b in chunk)
        )
        for job, tile in zip(chunk, tiles):
            run_job(job, tile, values)
        if step < len(rounds):
            running = jnp.sum(received[:, 0], axis=0)
            if step == 0:
                extra = received[:, 1]
            elif step == 1:
                row_coef = received[:, 1:].transpose(1, 0, 2, 3).reshape(row, probe_count, skeleton)
                extra = jnp.concatenate([row_coef[:COUPLE_REACH], row_coef[row - COUPLE_REACH :]])
            else:
                ends_coef = received[:, 1:]
    incoming = lax.ppermute(
        jnp.stack([outgoing[job] for job in cross]),
        GROUP_DEV,
        [(i, i + 1) for i in range(lax.axis_size(GROUP_DEV) - 1)],
    )
    for k, (a, b) in enumerate(cross):
        t = b - NEAR_REACH - leaf_count
        near[t] = near[t] + incoming[k] * pattern[t, NEAR_REACH - (b - a)]
    near = jnp.stack(near)

    own_skeleton = lax.dynamic_index_in_dim(group_skeleton, group_index, 0, keepdims=False)
    group_tiles = matern(
        group_skeleton.transpose(1, 0, 2).reshape(3, group_total * skeleton),
        own_skeleton,
        signal_variance,
    )
    others = lax.broadcasted_iota(jnp.int32, (group_total, 1, 1), 0) != group_index
    group_stack = jnp.where(others, group_coef, jnp.zeros_like(group_coef))
    group_stack = group_stack.transpose(1, 0, 2).reshape(probe_count, group_total * skeleton)
    far_group = jnp.dot(group_stack, group_tiles, preferred_element_type=f32)
    group_local = far_group.astype(jnp.bfloat16)

    own_node = lax.dynamic_index_in_dim(node_skeleton, node_index, 0, keepdims=False)
    ends = ends_coef.shape[1]
    table = jnp.concatenate([row_coef, ends_coef.reshape(-1, probe_count, skeleton)])
    line = node_index // row
    lines = lax.axis_size("dev_0")
    partner_points, picks, usable = [], [], []
    for offset in range(-COUPLE_REACH, COUPLE_REACH + 1):
        if abs(offset) < 2:
            continue
        partner = node_index + offset
        usable.append(
            (partner >= 0) & (partner < node_total) & (node_coupling[0, offset + COUPLE_REACH] > 0)
        )
        clamped = jnp.clip(partner, 0, node_total - 1)
        partner_points.append(lax.dynamic_index_in_dim(node_skeleton, clamped, 0, keepdims=False))
        along = node_index % row + offset
        same = jnp.clip(along, 0, row - 1)
        below = row + jnp.clip(line - 1, 0, lines - 1) * ends + COUPLE_REACH
        below = below + jnp.clip(along + COUPLE_REACH, 0, COUPLE_REACH - 1)
        above = row + jnp.clip(line + 1, 0, lines - 1) * ends
        above = above + jnp.clip(along - row, 0, COUPLE_REACH - 1)
        picks.append(jnp.where(along < 0, below, jnp.where(along >= row, above, same)))
    picked = jnp.take(table, jnp.stack(picks), axis=0)
    picked = jnp.where(jnp.stack(usable)[:, None, None], picked, jnp.zeros_like(picked))
    picked = picked.astype(jnp.bfloat16).transpose(1, 0, 2).reshape(probe_count, -1)
    couple_tiles = matern(jnp.concatenate(partner_points, axis=1), own_node, signal_variance)
    far_node = jnp.dot(picked, couple_tiles, preferred_element_type=f32)

    pushed = lax.dot_general(
        group_local, group_transfer[0], (((1,), (1,)), ((), ())), preferred_element_type=f32
    )
    node_local = (pushed + far_node).astype(jnp.bfloat16)
    spread = lax.dot_general(
        node_local, transfer_flat, (((1,), (1,)), ((), ())), preferred_element_type=f32
    )
    leaf_local = (
        spread.reshape(probe_count, leaf_count, skeleton).transpose(1, 0, 2).astype(jnp.bfloat16)
    )
    far_leaf = lax.dot_general(
        leaf_local, leaf_basis, (((2,), (2,)), ((0,), (0,))), preferred_element_type=f32
    )
    result = (far_leaf + near + noise_variance * ordered.astype(f32)).astype(jnp.bfloat16)
    restored = lax.dot_general(
        result, hots, (((2,), (2,)), ((0,), (0,))), preferred_element_type=f32
    )
    return restored.astype(jnp.bfloat16)


def solution(mesh):
    finer = Mesh(mesh.devices.reshape(mesh.shape["group"], 4, 4, 4), GROUP_DEV)
    return jax.shard_map(
        on_device,
        mesh=finer,
        in_specs=(
            P(GROUP_DEV, None, None),
            P(GROUP_DEV, None, None),
            P(GROUP_DEV, None),
            P(GROUP_DEV, None, None),
            P(GROUP_DEV, None, None, None),
            P(GROUP_DEV, None, None),
            P("group", None, None),
            P(),
            P(GROUP_DEV, None),
            P(GROUP_DEV, None),
            P(),
            P(),
        ),
        out_specs=P(GROUP_DEV, None, None),
        check_vma=False,
    )
```
